128 devices in a mesh: gz: 64 (over x_hi, z, y, core), row: 2 (over x_lo).
Axes of the slice: x: 4 (x_hi: 2, x_lo: 2; x = x_hi * 2 + x_lo), y: 4, z: 4, core: 2. Of those that a mesh axis runs over, the one named last changes fastest.
Arguments:
- axial_vel: float32 [1024, 256, 256], P('gz', 'row'), may hold values from -6 to 6
- radial_vel: float32 [1024, 256, 256], P('gz', 'row'), may hold values from -6 to 6
- swirl_vel: float32 [1024, 256, 256], P('gz', 'row'), may hold values from -6 to 6
- inflow_rate: float32 [48], replicated, may hold values from 0.25 to 2
- canopy_gore: int32 [1024, 256, 256], P('gz', 'row'), may hold values from 0 to 48, as said below
Outputs:
- axial_out: float32 [1024, 256, 256], P('gz', 'row')
- radial_projected_velocity: float32 [1024, 256, 256], P('gz', 'row')
- swirl_out: float32 [1024, 256, 256], P('gz', 'row')
The draws below stay inside these ranges and needn't reach their ends.
Inputs may be any that keep to these rules, and one draw needn't show every extreme that they name: `canopy_gore`: a canopy cell in azimuthal column t holds gore floor(t * 48 / 256); other cells hold 48.
All inputs are finite; a program needn't handle non-finite values.
Results may differ from the reference program's by a relative error of at most 0.0009.
Values sent between devices are 32-bit elements; how exact they have to be, the bound alone decides.
No kernel may reach another device: no remote copies, remote signals or barrier semaphores. Data moves between devices by JAX's collectives and lax.ppermute only.
A program may use at most 64 MiB of HBM per device.

```python
import math
import jax
import jax.numpy as jnp
from jax import lax

NX = 1024
NR = 256
NT = 256
GORES = 48


def draw_canopy_gore(key, part):
    cover = jax.random.randint(key, (NX, NR, NT), 0, 4)
    column = jnp.arange(NT, dtype=jnp.int32) * GORES // NT
    column = jnp.broadcast_to(column[None, None, :], (NX, NR, NT))
    return jnp.where(cover == 0, column, GORES).astype(jnp.int32)


def block_levels(rng, dims, cuts, least, largest):
    gain = 1.0
    for position, parts in cuts:
        heights = jax.random.uniform(jax.random.fold_in(jax.random.fold_in(rng, 6), position), (parts,), jnp.float32, least / len(cuts), largest / len(cuts))
        gain = gain * jnp.repeat(jnp.exp(heights), dims[position] // parts).reshape((-1,) + (1,) * (len(dims) - 1 - position))
    return gain


def normal_values(key, dims, deviation, bound, pieces=(), held_as=jnp.bfloat16):
    values = deviation * jax.random.normal(key, dims, jnp.float32)
    if pieces:
        values = values * block_levels(key, dims, pieces, -0.22, 0.18)
    return jnp.clip(values, -bound, bound).astype(held_as)


def setup_inputs(seed: int = 0) -> dict:
    splits = jax.random.split(jax.random.key(seed), 6)
    axial_vel = normal_values(splits[0], (NX, NR, NT), 1.0, 6.0, ((0, 64), (1, 2)), jnp.float32)
    radial_vel = normal_values(splits[1], (NX, NR, NT), 1.0, 6.0, ((0, 64), (1, 2)), jnp.float32)
    swirl_vel = normal_values(splits[2], (NX, NR, NT), 1.0, 6.0, ((0, 64), (1, 2)), jnp.float32)
    inflow_rate = jnp.clip(jnp.exp(jax.random.uniform(splits[3], (GORES,), jnp.float32, math.log(0.25), math.log(2.0))), 0.25, 2.0)
    canopy_gore = draw_canopy_gore(jax.random.fold_in(splits[5], 71), 0)
    return dict(axial_vel=axial_vel, radial_vel=radial_vel, swirl_vel=swirl_vel, inflow_rate=inflow_rate, canopy_gore=canopy_gore)


helmholtz_shift = 0.001
maximal_precision = lax.Precision.HIGHEST

def azimuth_basis(extent, mode_ids):
    positions = jnp.arange(extent, dtype=jnp.int32)
    half_way = extent // 2
    frequency = jnp.where(mode_ids <= half_way, mode_ids, mode_ids - half_way)
    phases = positions[:, None] * frequency[None, :] % extent
    angles = phases.astype(jnp.float32) * (2.0 * math.pi / extent)
    weights = jnp.where((mode_ids == 0) | (mode_ids == half_way), math.sqrt(1.0 / extent), math.sqrt(2.0 / extent)).astype(jnp.float32)
    return jnp.where((mode_ids > half_way)[None, :], jnp.sin(angles), jnp.cos(angles)) * weights[None, :]

def azimuth_eigen(mode_ids):
    half_way = NT // 2
    frequency = jnp.where(mode_ids <= half_way, mode_ids, mode_ids - half_way)
    angles = frequency.astype(jnp.float32) * (2.0 * math.pi / NT)
    arc_step = 0.75 * NR * 2.0 * math.pi / NT
    return (2.0 - 2.0 * jnp.cos(angles)) / (arc_step * arc_step)

def axial_basis(extent):
    indices = jnp.arange(extent, dtype=jnp.int32) + 1
    phases = indices[:, None] * indices[None, :] % (2 * (extent + 1))
    angles = phases.astype(jnp.float32) * (math.pi / (extent + 1))
    return jnp.sin(angles) * math.sqrt(2.0 / (extent + 1))

def axial_eigen(extent):
    indices = jnp.arange(extent, dtype=jnp.int32) + 1
    return 2.0 - 2.0 * jnp.cos(indices.astype(jnp.float32) * (math.pi / (extent + 1)))

def radial_basis(extent):
    mode_ids = jnp.arange(extent, dtype=jnp.int32)[:, None]
    cell_ids = jnp.arange(extent, dtype=jnp.int32)[None, :]
    phases = mode_ids * (2 * cell_ids + 1) % (4 * extent)
    angles = phases.astype(jnp.float32) * (math.pi / (2 * extent))
    weights = jnp.where(mode_ids == 0, math.sqrt(1.0 / extent), math.sqrt(2.0 / extent)).astype(jnp.float32)
    return jnp.cos(angles) * weights

def radial_eigen(mode_ids):
    return 2.0 - 2.0 * jnp.cos(mode_ids.astype(jnp.float32) * (math.pi / NR))

def cell_radius(cell_ids):
    return cell_ids.astype(jnp.float32) + (0.25 * NR + 0.5)

def reference(axial_vel, radial_vel, swirl_vel, inflow_rate, canopy_gore):
    spacing = 2.0 * math.pi / NT
    radius = cell_radius(jnp.arange(NR, dtype=jnp.int32))[None, :, None]
    axial_pad = jnp.pad(axial_vel, ((1, 1), (0, 0), (0, 0)))
    radial_flux = jnp.pad(radial_vel * radius, ((0, 0), (1, 1), (0, 0)))
    divergence = 0.5 * (axial_pad[2:] - axial_pad[:-2])
    divergence = divergence + (radial_flux[:, 2:] - radial_flux[:, :-2]) / (2.0 * radius)
    divergence = divergence + (jnp.roll(swirl_vel, -1, 2) - jnp.roll(swirl_vel, 1, 2)) / (2.0 * radius * spacing)
    rate_table = jnp.concatenate([inflow_rate, jnp.zeros((1,), jnp.float32)])
    right_side = divergence - jnp.take(rate_table, canopy_gore)
    all_modes = jnp.arange(NT, dtype=jnp.int32)
    fourier = azimuth_basis(NT, all_modes)
    axial_lookup_table = axial_basis(NX)
    radial_table = radial_basis(NR)
    spectrum = jnp.einsum('ijt,tm->mij', right_side, fourier, precision=maximal_precision)
    spectrum = jnp.einsum('ki,mij->mkj', axial_lookup_table, spectrum, precision=maximal_precision)
    spectrum = jnp.einsum('sj,mkj->mks', radial_table, spectrum, precision=maximal_precision)
    denominator = azimuth_eigen(all_modes)[:, None, None] + axial_eigen(NX)[None, :, None]
    denominator = denominator + radial_eigen(jnp.arange(NR, dtype=jnp.int32))[None, None, :] + helmholtz_shift
    scaled = spectrum / denominator
    scaled = jnp.einsum('sj,mks->mkj', radial_table, scaled, precision=maximal_precision)
    scaled = jnp.einsum('ki,mkj->mij', axial_lookup_table, scaled, precision=maximal_precision)
    pressure = -jnp.einsum('mij,tm->ijt', scaled, fourier, precision=maximal_precision)
    axial_p = jnp.pad(pressure, ((1, 1), (0, 0), (0, 0)))
    radial_p = jnp.pad(pressure, ((0, 0), (1, 1), (0, 0)), mode='edge')
    axial_out = axial_vel - 0.5 * (axial_p[2:] - axial_p[:-2])
    radial_projected_velocity = radial_vel - 0.5 * (radial_p[:, 2:] - radial_p[:, :-2])
    swirl_out = swirl_vel - (jnp.roll(pressure, -1, 2) - jnp.roll(pressure, 1, 2)) / (2.0 * radius * spacing)
    return (axial_out, radial_projected_velocity, swirl_out)
```

```python
import math

import jax
import jax.numpy as jnp
from jax import lax
from jax.sharding import PartitionSpec as P

NX = 1024
NR = 256
NT = 256
GORES = 48


helmholtz_shift = 0.001
maximal_precision = lax.Precision.HIGHEST


def extended(block, sides, width):
    for axis, dim in sides:
        count = lax.axis_size(axis)
        forward = [(i, i + 1) for i in range(count - 1)]
        backward = [(target, source) for source, target in forward]
        low = lax.ppermute(
            lax.slice_in_dim(block, block.shape[dim] - width, None, axis=dim), axis, forward
        )
        high = lax.ppermute(lax.slice_in_dim(block, 0, width, axis=dim), axis, backward)
        block = jnp.concatenate([low, block, high], axis=dim)
    return block


def azimuth_basis(extent, mode_ids):
    positions = jnp.arange(extent, dtype=jnp.int32)
    half_way = extent // 2
    frequency = jnp.where(mode_ids <= half_way, mode_ids, mode_ids - half_way)
    phases = positions[:, None] * frequency[None, :] % extent
    angles = phases.astype(jnp.float32) * (2.0 * math.pi / extent)
    weights = jnp.where(
        (mode_ids == 0) | (mode_ids == half_way), math.sqrt(1.0 / extent), math.sqrt(2.0 / extent)
    ).astype(jnp.float32)
    return (
        jnp.where((mode_ids > half_way)[None, :], jnp.sin(angles), jnp.cos(angles))
        * weights[None, :]
    )


def azimuth_eigen(mode_ids):
    half_way = NT // 2
    frequency = jnp.where(mode_ids <= half_way, mode_ids, mode_ids - half_way)
    angles = frequency.astype(jnp.float32) * (2.0 * math.pi / NT)
    arc_step = 0.75 * NR * 2.0 * math.pi / NT
    return (2.0 - 2.0 * jnp.cos(angles)) / (arc_step * arc_step)


def axial_basis(extent):
    indices = jnp.arange(extent, dtype=jnp.int32) + 1
    phases = indices[:, None] * indices[None, :] % (2 * (extent + 1))
    angles = phases.astype(jnp.float32) * (math.pi / (extent + 1))
    return jnp.sin(angles) * math.sqrt(2.0 / (extent + 1))


def axial_eigen(extent):
    indices = jnp.arange(extent, dtype=jnp.int32) + 1
    return 2.0 - 2.0 * jnp.cos(indices.astype(jnp.float32) * (math.pi / (extent + 1)))


def radial_basis(extent):
    mode_ids = jnp.arange(extent, dtype=jnp.int32)[:, None]
    cell_ids = jnp.arange(extent, dtype=jnp.int32)[None, :]
    phases = mode_ids * (2 * cell_ids + 1) % (4 * extent)
    angles = phases.astype(jnp.float32) * (math.pi / (2 * extent))
    weights = jnp.where(mode_ids == 0, math.sqrt(1.0 / extent), math.sqrt(2.0 / extent)).astype(
        jnp.float32
    )
    return jnp.cos(angles) * weights


def radial_eigen(mode_ids):
    return 2.0 - 2.0 * jnp.cos(mode_ids.astype(jnp.float32) * (math.pi / NR))


def cell_radius(cell_ids):
    return cell_ids.astype(jnp.float32) + (0.25 * NR + 0.5)


def denominator_of(mode_ids, radial_ids):
    total = azimuth_eigen(mode_ids)[:, None, None] + axial_eigen(NX)[None, :, None]
    return total + radial_eigen(radial_ids)[None, None, :] + helmholtz_shift


def canopy_source(gore_map, rate_table):
    gore_ids = jnp.arange(rate_table.shape[0], dtype=jnp.int32)
    column_gore = jnp.arange(NT, dtype=jnp.int32) * GORES // NT
    matches = column_gore[:, None] == gore_ids[None, :]
    column_rate = jnp.sum(jnp.where(matches, rate_table[None, :], 0.0), axis=1)
    return jnp.where(gore_map < GORES, column_rate[None, None, :], 0.0)


def body(axial_vel, radial_vel, swirl_vel, inflow_rate, canopy_gore):
    radial_block = axial_vel.shape[1]
    axial_block = axial_vel.shape[0]
    row_index = lax.axis_index("row")
    row_count = lax.axis_size("row")
    gz_count = lax.axis_size("gz")
    both = ("gz", "row")
    device_count = gz_count * row_count
    spacing = 2.0 * math.pi / NT
    own_first = row_index * radial_block
    own_cells = own_first + jnp.arange(radial_block, dtype=jnp.int32)
    radius = cell_radius(own_cells)[None, :, None]
    axial_pad = extended(axial_vel, (("gz", 0),), 1)
    radial_flux = extended(radial_vel * radius, (("row", 1),), 1)
    divergence = 0.5 * (axial_pad[2:] - axial_pad[:-2])
    divergence = divergence + (radial_flux[:, 2:] - radial_flux[:, :-2]) / (2.0 * radius)
    divergence = divergence + (jnp.roll(swirl_vel, -1, 2) - jnp.roll(swirl_vel, 1, 2)) / (
        2.0 * radius * spacing
    )
    right_side = divergence - canopy_source(canopy_gore, inflow_rate)
    all_modes = jnp.arange(NT, dtype=jnp.int32)
    fourier = azimuth_basis(NT, all_modes)
    spectrum_in = jnp.einsum("xrt,tm->mxr", right_side, fourier, precision=maximal_precision)
    modes_each = NT // device_count
    spectrum_in = spectrum_in.reshape(device_count, modes_each, axial_block, radial_block)
    resident = lax.all_to_all(spectrum_in, both, split_axis=0, concat_axis=0, tiled=True)
    resident = resident.reshape(gz_count, row_count, modes_each, axial_block, radial_block)
    mode_ids = lax.axis_index(both) * modes_each + jnp.arange(modes_each, dtype=jnp.int32)
    axial_table = axial_basis(NX).reshape(NX, gz_count, axial_block)
    radial_table = radial_basis(NR)
    axial_coefficient = jnp.einsum(
        "kgx,grmxj->mkrj", axial_table, resident, precision=maximal_precision
    ).reshape(modes_each, NX, NR)
    spectrum = jnp.einsum("sj,mkj->mks", radial_table, axial_coefficient, precision=maximal_precision)
    scaled = spectrum / denominator_of(mode_ids, jnp.arange(NR, dtype=jnp.int32))
    radial_returned = jnp.einsum("sj,mks->mkj", radial_table, scaled, precision=maximal_precision)
    radial_returned = radial_returned.reshape(modes_each, NX, row_count, radial_block)
    physical_space = jnp.einsum(
        "kgx,mkrj->grmxj", axial_table, radial_returned, precision=maximal_precision
    ).reshape(device_count, modes_each, axial_block, radial_block)
    returned = lax.all_to_all(physical_space, both, split_axis=0, concat_axis=0, tiled=True)
    returned = returned.reshape(NT, axial_block, radial_block)
    pressure = -jnp.einsum("qxr,tq->xrt", returned, fourier, precision=maximal_precision)
    padded = extended(pressure, (("gz", 0), ("row", 1)), 1)
    lower_ghost = jnp.where(row_index == 0, pressure[:, :1], padded[1:-1, :1])
    upper_ghost = jnp.where(row_index == row_count - 1, pressure[:, -1:], padded[1:-1, -1:])
    above = jnp.concatenate([pressure[:, 1:], upper_ghost], axis=1)
    below = jnp.concatenate([lower_ghost, pressure[:, :-1]], axis=1)
    axial_out = axial_vel - 0.5 * (padded[2:, 1:-1] - padded[:-2, 1:-1])
    radial_projected_velocity = radial_vel - 0.5 * (above - below)
    swirl_out = swirl_vel - (jnp.roll(pressure, -1, 2) - jnp.roll(pressure, 1, 2)) / (
        2.0 * radius * spacing
    )
    return (axial_out, radial_projected_velocity, swirl_out)


def solution(mesh):
    placed = (
        P("gz", "row", None),
        P("gz", "row", None),
        P("gz", "row", None),
        P(),
        P("gz", "row", None),
    )
    return jax.shard_map(
        body,
        mesh=mesh,
        in_specs=placed,
        out_specs=(P("gz", "row", None), P("gz", "row", None), P("gz", "row", None)),
        check_vma=False,
    )
```

```python
import math

import jax
import jax.numpy as jnp
from jax import lax
from jax.sharding import PartitionSpec as P

NX = 1024
NR = 256
NT = 256
GORES = 48


helmholtz_shift = 0.001
maximal_precision = lax.Precision.HIGHEST
transform_precision = lax.Precision.HIGHEST


def extended(block, sides, width):
    for axis, dim in sides:
        count = lax.axis_size(axis)
        forward = [(i, i + 1) for i in range(count - 1)]
        backward = [(target, source) for source, target in forward]
        low = lax.ppermute(
            lax.slice_in_dim(block, block.shape[dim] - width, None, axis=dim), axis, forward
        )
        high = lax.ppermute(lax.slice_in_dim(block, 0, width, axis=dim), axis, backward)
        block = jnp.concatenate([low, block, high], axis=dim)
    return block


def azimuth_basis(extent, mode_ids):
    positions = jnp.arange(extent, dtype=jnp.int32)
    half_way = extent // 2
    frequency = jnp.where(mode_ids <= half_way, mode_ids, mode_ids - half_way)
    phases = positions[:, None] * frequency[None, :] % extent
    angles = phases.astype(jnp.float32) * (2.0 * math.pi / extent)
    weights = jnp.where(
        (mode_ids == 0) | (mode_ids == half_way), math.sqrt(1.0 / extent), math.sqrt(2.0 / extent)
    ).astype(jnp.float32)
    return (
        jnp.where((mode_ids > half_way)[None, :], jnp.sin(angles), jnp.cos(angles))
        * weights[None, :]
    )


def azimuth_eigen(mode_ids):
    half_way = NT // 2
    frequency = jnp.where(mode_ids <= half_way, mode_ids, mode_ids - half_way)
    angles = frequency.astype(jnp.float32) * (2.0 * math.pi / NT)
    arc_step = 0.75 * NR * 2.0 * math.pi / NT
    return (2.0 - 2.0 * jnp.cos(angles)) / (arc_step * arc_step)


def axial_basis(extent):
    indices = jnp.arange(extent, dtype=jnp.int32) + 1
    phases = indices[:, None] * indices[None, :] % (2 * (extent + 1))
    angles = phases.astype(jnp.float32) * (math.pi / (extent + 1))
    return jnp.sin(angles) * math.sqrt(2.0 / (extent + 1))


def axial_eigen(extent):
    indices = jnp.arange(extent, dtype=jnp.int32) + 1
    return 2.0 - 2.0 * jnp.cos(indices.astype(jnp.float32) * (math.pi / (extent + 1)))


def radial_basis(extent):
    mode_ids = jnp.arange(extent, dtype=jnp.int32)[:, None]
    cell_ids = jnp.arange(extent, dtype=jnp.int32)[None, :]
    phases = mode_ids * (2 * cell_ids + 1) % (4 * extent)
    angles = phases.astype(jnp.float32) * (math.pi / (2 * extent))
    weights = jnp.where(mode_ids == 0, math.sqrt(1.0 / extent), math.sqrt(2.0 / extent)).astype(
        jnp.float32
    )
    return jnp.cos(angles) * weights


def radial_eigen(mode_ids):
    return 2.0 - 2.0 * jnp.cos(mode_ids.astype(jnp.float32) * (math.pi / NR))


def cell_radius(cell_ids):
    return cell_ids.astype(jnp.float32) + (0.25 * NR + 0.5)


def denominator_of(mode_ids, radial_ids):
    total = azimuth_eigen(mode_ids)[:, None, None] + axial_eigen(NX)[None, :, None]
    return total + radial_eigen(radial_ids)[None, None, :] + helmholtz_shift


def canopy_source(gore_map, rate_table):
    gore_ids = jnp.arange(rate_table.shape[0], dtype=jnp.int32)
    column_gore = jnp.arange(NT, dtype=jnp.int32) * GORES // NT
    matches = column_gore[:, None] == gore_ids[None, :]
    column_rate = jnp.sum(jnp.where(matches, rate_table[None, :], 0.0), axis=1)
    return jnp.where(gore_map < GORES, column_rate[None, None, :], 0.0)


def body(axial_vel, radial_vel, swirl_vel, inflow_rate, canopy_gore):
    radial_block = axial_vel.shape[1]
    axial_block = axial_vel.shape[0]
    row_index = lax.axis_index("row")
    row_count = lax.axis_size("row")
    gz_count = lax.axis_size("gz")
    both = ("gz", "row")
    device_count = gz_count * row_count
    spacing = 2.0 * math.pi / NT
    own_first = row_index * radial_block
    own_cells = own_first + jnp.arange(radial_block, dtype=jnp.int32)
    radius = cell_radius(own_cells)[None, :, None]
    axial_pad = extended(axial_vel, (("gz", 0),), 1)
    radial_flux = extended(radial_vel * radius, (("row", 1),), 1)
    divergence = 0.5 * (axial_pad[2:] - axial_pad[:-2])
    divergence = divergence + (radial_flux[:, 2:] - radial_flux[:, :-2]) / (2.0 * radius)
    divergence = divergence + (jnp.roll(swirl_vel, -1, 2) - jnp.roll(swirl_vel, 1, 2)) / (
        2.0 * radius * spacing
    )
    right_side = divergence - canopy_source(canopy_gore, inflow_rate)
    all_modes = jnp.arange(NT, dtype=jnp.int32)
    fourier = azimuth_basis(NT, all_modes)
    spectrum_in = jnp.einsum("xrt,tm->mxr", right_side, fourier, precision=transform_precision)
    modes_each = NT // device_count
    spectrum_in = spectrum_in.reshape(device_count, modes_each, axial_block, radial_block)
    resident = lax.all_to_all(spectrum_in, both, split_axis=0, concat_axis=0, tiled=True)
    resident = resident.reshape(gz_count, row_count, modes_each, axial_block, radial_block)
    mode_ids = lax.axis_index(both) * modes_each + jnp.arange(modes_each, dtype=jnp.int32)
    axial_table = axial_basis(NX)
    radial_table = radial_basis(NR)
    resident = resident.transpose(2, 0, 3, 1, 4).reshape(modes_each, NX, NR)
    axial_coefficient = jnp.einsum(
        "ki,min->mkn", axial_table, resident, precision=transform_precision
    )
    spectrum = jnp.einsum("sj,mkj->mks", radial_table, axial_coefficient, precision=transform_precision)
    scaled = spectrum / denominator_of(mode_ids, jnp.arange(NR, dtype=jnp.int32))
    radial_returned = jnp.einsum("sj,mks->mkj", radial_table, scaled, precision=transform_precision)
    physical_space = jnp.einsum(
        "ki,mkn->min", axial_table, radial_returned, precision=transform_precision
    )
    padded = jnp.pad(physical_space, ((0, 0), (1, 1), (0, 0)))
    padded = jnp.pad(padded, ((0, 0), (0, 0), (1, 1)), mode="edge")
    inner = padded[:, 1 : NX + 1].reshape(modes_each, gz_count, axial_block, NR + 2)
    lower = padded[:, 0:NX:axial_block][:, :, None]
    upper = padded[:, axial_block + 1 :: axial_block][:, :, None]
    windows = jnp.concatenate([lower, inner, upper], axis=2)
    windows = jnp.stack(
        [windows[..., r * radial_block : r * radial_block + radial_block + 2] for r in range(row_count)],
        axis=2,
    )
    windows = windows.transpose(1, 2, 0, 3, 4).reshape(device_count, -1)
    returned = lax.all_to_all(windows, both, split_axis=0, concat_axis=0, tiled=True)
    returned = returned.reshape(NT, axial_block + 2, radial_block + 2)
    extended_p = -jnp.einsum("qxr,tq->xrt", returned, fourier, precision=transform_precision)
    pressure = extended_p[1:-1, 1:-1]
    axial_out = axial_vel - 0.5 * (extended_p[2:, 1:-1] - extended_p[:-2, 1:-1])
    radial_projected_velocity = radial_vel - 0.5 * (extended_p[1:-1, 2:] - extended_p[1:-1, :-2])
    swirl_out = swirl_vel - (jnp.roll(pressure, -1, 2) - jnp.roll(pressure, 1, 2)) / (
        2.0 * radius * spacing
    )
    return (axial_out, radial_projected_velocity, swirl_out)


def solution(mesh):
    placed = (
        P("gz", "row", None),
        P("gz", "row", None),
        P("gz", "row", None),
        P(),
        P("gz", "row", None),
    )
    return jax.shard_map(
        body,
        mesh=mesh,
        in_specs=placed,
        out_specs=(P("gz", "row", None), P("gz", "row", None), P("gz", "row", None)),
        check_vma=False,
    )
```

```python
import math

import numpy as np

import jax
import jax.numpy as jnp
from jax import lax
from jax.sharding import PartitionSpec as P

NX = 1024
NR = 256
NT = 256
GORES = 48


helmholtz_shift = 0.001
maximal_precision = lax.Precision.HIGHEST


def extended(block, sides, width):
    for axis, dim in sides:
        count = lax.axis_size(axis)
        forward = [(i, i + 1) for i in range(count - 1)]
        backward = [(target, source) for source, target in forward]
        low = lax.ppermute(
            lax.slice_in_dim(block, block.shape[dim] - width, None, axis=dim), axis, forward
        )
        high = lax.ppermute(lax.slice_in_dim(block, 0, width, axis=dim), axis, backward)
        block = jnp.concatenate([low, block, high], axis=dim)
    return block


def azimuth_basis(extent, mode_ids):
    positions = jnp.arange(extent, dtype=jnp.int32)
    half_way = extent // 2
    frequency = jnp.where(mode_ids <= half_way, mode_ids, mode_ids - half_way)
    phases = positions[:, None] * frequency[None, :] % extent
    angles = phases.astype(jnp.float32) * (2.0 * math.pi / extent)
    weights = jnp.where(
        (mode_ids == 0) | (mode_ids == half_way), math.sqrt(1.0 / extent), math.sqrt(2.0 / extent)
    ).astype(jnp.float32)
    return (
        jnp.where((mode_ids > half_way)[None, :], jnp.sin(angles), jnp.cos(angles))
        * weights[None, :]
    )


def azimuth_eigen(mode_ids):
    half_way = NT // 2
    frequency = jnp.where(mode_ids <= half_way, mode_ids, mode_ids - half_way)
    angles = frequency.astype(jnp.float32) * (2.0 * math.pi / NT)
    arc_step = 0.75 * NR * 2.0 * math.pi / NT
    return (2.0 - 2.0 * jnp.cos(angles)) / (arc_step * arc_step)


def axial_basis(extent):
    indices = jnp.arange(extent, dtype=jnp.int32) + 1
    phases = indices[:, None] * indices[None, :] % (2 * (extent + 1))
    angles = phases.astype(jnp.float32) * (math.pi / (extent + 1))
    return jnp.sin(angles) * math.sqrt(2.0 / (extent + 1))


def axial_eigen(extent):
    indices = jnp.arange(extent, dtype=jnp.int32) + 1
    return 2.0 - 2.0 * jnp.cos(indices.astype(jnp.float32) * (math.pi / (extent + 1)))


def radial_basis(extent):
    mode_ids = jnp.arange(extent, dtype=jnp.int32)[:, None]
    cell_ids = jnp.arange(extent, dtype=jnp.int32)[None, :]
    phases = mode_ids * (2 * cell_ids + 1) % (4 * extent)
    angles = phases.astype(jnp.float32) * (math.pi / (2 * extent))
    weights = jnp.where(mode_ids == 0, math.sqrt(1.0 / extent), math.sqrt(2.0 / extent)).astype(
        jnp.float32
    )
    return jnp.cos(angles) * weights


def radial_eigen(mode_ids):
    return 2.0 - 2.0 * jnp.cos(mode_ids.astype(jnp.float32) * (math.pi / NR))


def cell_radius(cell_ids):
    return cell_ids.astype(jnp.float32) + (0.25 * NR + 0.5)


def fixed_azimuth_basis():
    positions = np.arange(NT)[:, None]
    modes = np.arange(NT)[None, :]
    frequency = np.where(modes <= NT // 2, modes, modes - NT // 2)
    angles = (positions * frequency % NT) * (2.0 * math.pi / NT)
    weights = np.where((modes == 0) | (modes == NT // 2), math.sqrt(1.0 / NT), math.sqrt(2.0 / NT))
    return (np.where(modes > NT // 2, np.sin(angles), np.cos(angles)) * weights).astype(np.float32)


def fixed_axial_basis():
    indices = np.arange(1, NX + 1)
    phases = indices[:, None] * indices[None, :] % (2 * (NX + 1))
    return (np.sin(phases * (math.pi / (NX + 1))) * math.sqrt(2.0 / (NX + 1))).astype(np.float32)


def fixed_radial_basis():
    modes = np.arange(NR)[:, None]
    cells = np.arange(NR)[None, :]
    angles = (modes * (2 * cells + 1) % (4 * NR)) * (math.pi / (2 * NR))
    weights = np.where(modes == 0, math.sqrt(1.0 / NR), math.sqrt(2.0 / NR))
    return (np.cos(angles) * weights).astype(np.float32)


AZIMUTH_TABLE = fixed_azimuth_basis()
AXIAL_TABLE = fixed_axial_basis()
RADIAL_TABLE = fixed_radial_basis()


def denominator_of(mode_ids, radial_ids):
    total = azimuth_eigen(mode_ids)[:, None, None] + axial_eigen(NX)[None, :, None]
    return total + radial_eigen(radial_ids)[None, None, :] + helmholtz_shift


def canopy_source(gore_map, rate_table):
    gore_ids = jnp.arange(rate_table.shape[0], dtype=jnp.int32)
    column_gore = jnp.arange(NT, dtype=jnp.int32) * GORES // NT
    matches = column_gore[:, None] == gore_ids[None, :]
    column_rate = jnp.sum(jnp.where(matches, rate_table[None, :], 0.0), axis=1)
    return jnp.where(gore_map < GORES, column_rate[None, None, :], 0.0)


def body(axial_vel, radial_vel, swirl_vel, inflow_rate, canopy_gore):
    radial_block = axial_vel.shape[1]
    axial_block = axial_vel.shape[0]
    row_index = lax.axis_index("row")
    row_count = lax.axis_size("row")
    gz_count = lax.axis_size("gz")
    both = ("gz", "row")
    device_count = gz_count * row_count
    spacing = 2.0 * math.pi / NT
    own_first = row_index * radial_block
    own_cells = own_first + jnp.arange(radial_block, dtype=jnp.int32)
    radius = cell_radius(own_cells)[None, :, None]
    axial_pad = extended(axial_vel, (("gz", 0),), 1)
    radial_flux = extended(radial_vel * radius, (("row", 1),), 1)
    divergence = 0.5 * (axial_pad[2:] - axial_pad[:-2])
    divergence = divergence + (radial_flux[:, 2:] - radial_flux[:, :-2]) / (2.0 * radius)
    divergence = divergence + (jnp.roll(swirl_vel, -1, 2) - jnp.roll(swirl_vel, 1, 2)) / (
        2.0 * radius * spacing
    )
    right_side = divergence - canopy_source(canopy_gore, inflow_rate)
    all_modes = jnp.arange(NT, dtype=jnp.int32)
    fourier = jnp.asarray(AZIMUTH_TABLE)
    spectrum_in = jnp.einsum("xrt,tm->mxr", right_side, fourier, precision=maximal_precision)
    modes_each = NT // device_count
    spectrum_in = spectrum_in.reshape(device_count, modes_each, axial_block, radial_block)
    resident = lax.all_to_all(spectrum_in, both, split_axis=0, concat_axis=0, tiled=True)
    resident = resident.reshape(gz_count, row_count, modes_each, axial_block, radial_block)
    mode_ids = lax.axis_index(both) * modes_each + jnp.arange(modes_each, dtype=jnp.int32)
    axial_table = jnp.asarray(AXIAL_TABLE).reshape(NX, gz_count, axial_block)
    radial_table = jnp.asarray(RADIAL_TABLE)
    axial_coefficient = jnp.einsum(
        "kgx,grmxj->mkrj", axial_table, resident, precision=maximal_precision
    ).reshape(modes_each, NX, NR)
    spectrum = jnp.einsum("sj,mkj->mks", radial_table, axial_coefficient, precision=maximal_precision)
    scaled = spectrum / denominator_of(mode_ids, jnp.arange(NR, dtype=jnp.int32))
    radial_returned = jnp.einsum("sj,mks->mkj", radial_table, scaled, precision=maximal_precision)
    radial_returned = radial_returned.reshape(modes_each, NX, row_count, radial_block)
    physical_space = jnp.einsum(
        "kgx,mkrj->grmxj", axial_table, radial_returned, precision=maximal_precision
    ).reshape(device_count, modes_each, axial_block, radial_block)
    returned = lax.all_to_all(physical_space, both, split_axis=0, concat_axis=0, tiled=True)
    returned = returned.reshape(NT, axial_block, radial_block)
    pressure = -jnp.einsum("qxr,tq->xrt", returned, fourier, precision=maximal_precision)
    padded = extended(pressure, (("gz", 0), ("row", 1)), 1)
    lower_ghost = jnp.where(row_index == 0, pressure[:, :1], padded[1:-1, :1])
    upper_ghost = jnp.where(row_index == row_count - 1, pressure[:, -1:], padded[1:-1, -1:])
    above = jnp.concatenate([pressure[:, 1:], upper_ghost], axis=1)
    below = jnp.concatenate([lower_ghost, pressure[:, :-1]], axis=1)
    axial_out = axial_vel - 0.5 * (padded[2:, 1:-1] - padded[:-2, 1:-1])
    radial_projected_velocity = radial_vel - 0.5 * (above - below)
    swirl_out = swirl_vel - (jnp.roll(pressure, -1, 2) - jnp.roll(pressure, 1, 2)) / (
        2.0 * radius * spacing
    )
    return (axial_out, radial_projected_velocity, swirl_out)


def solution(mesh):
    placed = (
        P("gz", "row", None),
        P("gz", "row", None),
        P("gz", "row", None),
        P(),
        P("gz", "row", None),
    )
    return jax.shard_map(
        body,
        mesh=mesh,
        in_specs=placed,
        out_specs=(P("gz", "row", None), P("gz", "row", None), P("gz", "row", None)),
        check_vma=False,
    )
```

```python
import math

import numpy as np

import jax
import jax.numpy as jnp
from jax import lax
from jax.sharding import PartitionSpec as P

NX = 1024
NR = 256
NT = 256
GORES = 48


helmholtz_shift = 0.001
maximal_precision = lax.Precision.HIGHEST


def extended(block, sides, width):
    for axis, dim in sides:
        count = lax.axis_size(axis)
        forward = [(i, i + 1) for i in range(count - 1)]
        backward = [(target, source) for source, target in forward]
        low = lax.ppermute(
            lax.slice_in_dim(block, block.shape[dim] - width, None, axis=dim), axis, forward
        )
        high = lax.ppermute(lax.slice_in_dim(block, 0, width, axis=dim), axis, backward)
        block = jnp.concatenate([low, block, high], axis=dim)
    return block


def azimuth_basis(extent, mode_ids):
    positions = jnp.arange(extent, dtype=jnp.int32)
    half_way = extent // 2
    frequency = jnp.where(mode_ids <= half_way, mode_ids, mode_ids - half_way)
    phases = positions[:, None] * frequency[None, :] % extent
    angles = phases.astype(jnp.float32) * (2.0 * math.pi / extent)
    weights = jnp.where(
        (mode_ids == 0) | (mode_ids == half_way), math.sqrt(1.0 / extent), math.sqrt(2.0 / extent)
    ).astype(jnp.float32)
    return (
        jnp.where((mode_ids > half_way)[None, :], jnp.sin(angles), jnp.cos(angles))
        * weights[None, :]
    )


def azimuth_eigen(mode_ids):
    half_way = NT // 2
    frequency = jnp.where(mode_ids <= half_way, mode_ids, mode_ids - half_way)
    angles = frequency.astype(jnp.float32) * (2.0 * math.pi / NT)
    arc_step = 0.75 * NR * 2.0 * math.pi / NT
    return (2.0 - 2.0 * jnp.cos(angles)) / (arc_step * arc_step)


def axial_basis(extent):
    indices = jnp.arange(extent, dtype=jnp.int32) + 1
    phases = indices[:, None] * indices[None, :] % (2 * (extent + 1))
    angles = phases.astype(jnp.float32) * (math.pi / (extent + 1))
    return jnp.sin(angles) * math.sqrt(2.0 / (extent + 1))


def axial_eigen(extent):
    indices = jnp.arange(extent, dtype=jnp.int32) + 1
    return 2.0 - 2.0 * jnp.cos(indices.astype(jnp.float32) * (math.pi / (extent + 1)))


def radial_basis(extent):
    mode_ids = jnp.arange(extent, dtype=jnp.int32)[:, None]
    cell_ids = jnp.arange(extent, dtype=jnp.int32)[None, :]
    phases = mode_ids * (2 * cell_ids + 1) % (4 * extent)
    angles = phases.astype(jnp.float32) * (math.pi / (2 * extent))
    weights = jnp.where(mode_ids == 0, math.sqrt(1.0 / extent), math.sqrt(2.0 / extent)).astype(
        jnp.float32
    )
    return jnp.cos(angles) * weights


def radial_eigen(mode_ids):
    return 2.0 - 2.0 * jnp.cos(mode_ids.astype(jnp.float32) * (math.pi / NR))


def cell_radius(cell_ids):
    return cell_ids.astype(jnp.float32) + (0.25 * NR + 0.5)


def fixed_azimuth_basis():
    positions = np.arange(NT)[:, None]
    modes = np.arange(NT)[None, :]
    frequency = np.where(modes <= NT // 2, modes, modes - NT // 2)
    angles = (positions * frequency % NT) * (2.0 * math.pi / NT)
    weights = np.where((modes == 0) | (modes == NT // 2), math.sqrt(1.0 / NT), math.sqrt(2.0 / NT))
    return (np.where(modes > NT // 2, np.sin(angles), np.cos(angles)) * weights).astype(np.float32)


def fixed_axial_basis():
    indices = np.arange(1, NX + 1)
    phases = indices[:, None] * indices[None, :] % (2 * (NX + 1))
    return (np.sin(phases * (math.pi / (NX + 1))) * math.sqrt(2.0 / (NX + 1))).astype(np.float32)


def fixed_radial_basis():
    modes = np.arange(NR)[:, None]
    cells = np.arange(NR)[None, :]
    angles = (modes * (2 * cells + 1) % (4 * NR)) * (math.pi / (2 * NR))
    weights = np.where(modes == 0, math.sqrt(1.0 / NR), math.sqrt(2.0 / NR))
    return (np.cos(angles) * weights).astype(np.float32)


AZIMUTH_TABLE = fixed_azimuth_basis()
AXIAL_TABLE = fixed_axial_basis()
RADIAL_TABLE = fixed_radial_basis()


def denominator_of(mode_ids, radial_ids):
    total = azimuth_eigen(mode_ids)[:, None, None] + axial_eigen(NX)[None, :, None]
    return total + radial_eigen(radial_ids)[None, None, :] + helmholtz_shift


def canopy_source(gore_map, rate_table):
    gore_ids = jnp.arange(rate_table.shape[0], dtype=jnp.int32)
    column_gore = jnp.arange(NT, dtype=jnp.int32) * GORES // NT
    matches = column_gore[:, None] == gore_ids[None, :]
    column_rate = jnp.sum(jnp.where(matches, rate_table[None, :], 0.0), axis=1)
    return jnp.where(gore_map < GORES, column_rate[None, None, :], 0.0)


def body(axial_vel, radial_vel, swirl_vel, inflow_rate, canopy_gore):
    radial_block = axial_vel.shape[1]
    axial_block = axial_vel.shape[0]
    row_index = lax.axis_index("row")
    row_count = lax.axis_size("row")
    gz_count = lax.axis_size("gz")
    both = ("gz", "row")
    device_count = gz_count * row_count
    spacing = 2.0 * math.pi / NT
    own_first = row_index * radial_block
    own_cells = own_first + jnp.arange(radial_block, dtype=jnp.int32)
    radius = cell_radius(own_cells)[None, :, None]
    axial_pad = extended(axial_vel, (("gz", 0),), 1)
    radial_flux = extended(radial_vel * radius, (("row", 1),), 1)
    divergence = 0.5 * (axial_pad[2:] - axial_pad[:-2])
    divergence = divergence + (radial_flux[:, 2:] - radial_flux[:, :-2]) / (2.0 * radius)
    divergence = divergence + (jnp.roll(swirl_vel, -1, 2) - jnp.roll(swirl_vel, 1, 2)) / (
        2.0 * radius * spacing
    )
    right_side = divergence - canopy_source(canopy_gore, inflow_rate)
    all_modes = jnp.arange(NT, dtype=jnp.int32)
    fourier = jnp.asarray(AZIMUTH_TABLE)
    modes_each = NT // device_count
    mode_base = lax.axis_index(both) * modes_each
    axial_table = jnp.asarray(AXIAL_TABLE).reshape(NX, gz_count, axial_block)
    radial_table = jnp.asarray(RADIAL_TABLE)
    pressure = None
    for slot in range(modes_each):
        slot_basis = fourier[:, slot::modes_each]
        spectrum_in = jnp.einsum("xrt,tm->mxr", right_side, slot_basis, precision=maximal_precision)
        resident = lax.all_to_all(spectrum_in, both, split_axis=0, concat_axis=0, tiled=True)
        resident = resident.reshape(gz_count, row_count, axial_block, radial_block)
        mode_ids = (mode_base + slot)[None]
        axial_coefficient = jnp.einsum(
            "kgx,grxj->krj", axial_table, resident, precision=maximal_precision
        ).reshape(1, NX, NR)
        spectrum = jnp.einsum("sj,mkj->mks", radial_table, axial_coefficient, precision=maximal_precision)
        scaled = spectrum / denominator_of(mode_ids, jnp.arange(NR, dtype=jnp.int32))
        radial_returned = jnp.einsum("sj,mks->kj", radial_table, scaled, precision=maximal_precision)
        radial_returned = radial_returned.reshape(NX, row_count, radial_block)
        physical_space = jnp.einsum(
            "kgx,krj->grxj", axial_table, radial_returned, precision=maximal_precision
        ).reshape(device_count, axial_block, radial_block)
        returned = lax.all_to_all(physical_space, both, split_axis=0, concat_axis=0, tiled=True)
        part = -jnp.einsum("qxr,tq->xrt", returned, slot_basis, precision=maximal_precision)
        pressure = part if pressure is None else pressure + part
    padded = extended(pressure, (("gz", 0), ("row", 1)), 1)
    lower_ghost = jnp.where(row_index == 0, pressure[:, :1], padded[1:-1, :1])
    upper_ghost = jnp.where(row_index == row_count - 1, pressure[:, -1:], padded[1:-1, -1:])
    above = jnp.concatenate([pressure[:, 1:], upper_ghost], axis=1)
    below = jnp.concatenate([lower_ghost, pressure[:, :-1]], axis=1)
    axial_out = axial_vel - 0.5 * (padded[2:, 1:-1] - padded[:-2, 1:-1])
    radial_projected_velocity = radial_vel - 0.5 * (above - below)
    swirl_out = swirl_vel - (jnp.roll(pressure, -1, 2) - jnp.roll(pressure, 1, 2)) / (
        2.0 * radius * spacing
    )
    return (axial_out, radial_projected_velocity, swirl_out)


def solution(mesh):
    placed = (
        P("gz", "row", None),
        P("gz", "row", None),
        P("gz", "row", None),
        P(),
        P("gz", "row", None),
    )
    return jax.shard_map(
        body,
        mesh=mesh,
        in_specs=placed,
        out_specs=(P("gz", "row", None), P("gz", "row", None), P("gz", "row", None)),
        check_vma=False,
    )
```

```python
import math

import numpy as np

import jax
import jax.numpy as jnp
from jax import lax
from jax.sharding import PartitionSpec as P

NX = 1024
NR = 256
NT = 256
GORES = 48


helmholtz_shift = 0.001
maximal_precision = lax.Precision.HIGHEST


def extended(block, sides, width):
    for axis, dim in sides:
        count = lax.axis_size(axis)
        forward = [(i, i + 1) for i in range(count - 1)]
        backward = [(target, source) for source, target in forward]
        low = lax.ppermute(
            lax.slice_in_dim(block, block.shape[dim] - width, None, axis=dim), axis, forward
        )
        high = lax.ppermute(lax.slice_in_dim(block, 0, width, axis=dim), axis, backward)
        block = jnp.concatenate([low, block, high], axis=dim)
    return block


def radial_neighbour(block, ghost_low, ghost_high):
    row_index = lax.axis_index("row")
    send = jnp.where(row_index == 0, block[:, -1:], block[:, :1])
    received = lax.ppermute(send, "row", [(0, 1), (1, 0)])
    low = jnp.where(row_index == 0, ghost_low, received)
    high = jnp.where(row_index == 0, received, ghost_high)
    return jnp.concatenate([low, block, high], axis=1)


def azimuth_basis(extent, mode_ids):
    positions = jnp.arange(extent, dtype=jnp.int32)
    half_way = extent // 2
    frequency = jnp.where(mode_ids <= half_way, mode_ids, mode_ids - half_way)
    phases = positions[:, None] * frequency[None, :] % extent
    angles = phases.astype(jnp.float32) * (2.0 * math.pi / extent)
    weights = jnp.where(
        (mode_ids == 0) | (mode_ids == half_way), math.sqrt(1.0 / extent), math.sqrt(2.0 / extent)
    ).astype(jnp.float32)
    return (
        jnp.where((mode_ids > half_way)[None, :], jnp.sin(angles), jnp.cos(angles))
        * weights[None, :]
    )


def azimuth_eigen(mode_ids):
    half_way = NT // 2
    frequency = jnp.where(mode_ids <= half_way, mode_ids, mode_ids - half_way)
    angles = frequency.astype(jnp.float32) * (2.0 * math.pi / NT)
    arc_step = 0.75 * NR * 2.0 * math.pi / NT
    return (2.0 - 2.0 * jnp.cos(angles)) / (arc_step * arc_step)


def axial_basis(extent):
    indices = jnp.arange(extent, dtype=jnp.int32) + 1
    phases = indices[:, None] * indices[None, :] % (2 * (extent + 1))
    angles = phases.astype(jnp.float32) * (math.pi / (extent + 1))
    return jnp.sin(angles) * math.sqrt(2.0 / (extent + 1))


def axial_eigen(extent):
    indices = jnp.arange(extent, dtype=jnp.int32) + 1
    return 2.0 - 2.0 * jnp.cos(indices.astype(jnp.float32) * (math.pi / (extent + 1)))


def radial_basis(extent):
    mode_ids = jnp.arange(extent, dtype=jnp.int32)[:, None]
    cell_ids = jnp.arange(extent, dtype=jnp.int32)[None, :]
    phases = mode_ids * (2 * cell_ids + 1) % (4 * extent)
    angles = phases.astype(jnp.float32) * (math.pi / (2 * extent))
    weights = jnp.where(mode_ids == 0, math.sqrt(1.0 / extent), math.sqrt(2.0 / extent)).astype(
        jnp.float32
    )
    return jnp.cos(angles) * weights


def radial_eigen(mode_ids):
    return 2.0 - 2.0 * jnp.cos(mode_ids.astype(jnp.float32) * (math.pi / NR))


def cell_radius(cell_ids):
    return cell_ids.astype(jnp.float32) + (0.25 * NR + 0.5)


def fixed_azimuth_basis():
    positions = np.arange(NT)[:, None]
    modes = np.arange(NT)[None, :]
    frequency = np.where(modes <= NT // 2, modes, modes - NT // 2)
    angles = (positions * frequency % NT) * (2.0 * math.pi / NT)
    weights = np.where((modes == 0) | (modes == NT // 2), math.sqrt(1.0 / NT), math.sqrt(2.0 / NT))
    return (np.where(modes > NT // 2, np.sin(angles), np.cos(angles)) * weights).astype(np.float32)


def fixed_axial_basis():
    indices = np.arange(1, NX + 1)
    phases = indices[:, None] * indices[None, :] % (2 * (NX + 1))
    return (np.sin(phases * (math.pi / (NX + 1))) * math.sqrt(2.0 / (NX + 1))).astype(np.float32)


def fixed_radial_basis():
    modes = np.arange(NR)[:, None]
    cells = np.arange(NR)[None, :]
    angles = (modes * (2 * cells + 1) % (4 * NR)) * (math.pi / (2 * NR))
    weights = np.where(modes == 0, math.sqrt(1.0 / NR), math.sqrt(2.0 / NR))
    return (np.cos(angles) * weights).astype(np.float32)


AZIMUTH_TABLE = fixed_azimuth_basis()
AXIAL_TABLE = fixed_axial_basis()
RADIAL_TABLE = fixed_radial_basis()


def denominator_of(mode_ids, radial_ids):
    total = azimuth_eigen(mode_ids)[:, None, None] + axial_eigen(NX)[None, :, None]
    return total + radial_eigen(radial_ids)[None, None, :] + helmholtz_shift


def canopy_source(gore_map, rate_table):
    gore_ids = jnp.arange(rate_table.shape[0], dtype=jnp.int32)
    column_gore = jnp.arange(NT, dtype=jnp.int32) * GORES // NT
    matches = column_gore[:, None] == gore_ids[None, :]
    column_rate = jnp.sum(jnp.where(matches, rate_table[None, :], 0.0), axis=1)
    return jnp.where(gore_map < GORES, column_rate[None, None, :], 0.0)


def body(axial_vel, radial_vel, swirl_vel, inflow_rate, canopy_gore):
    radial_block = axial_vel.shape[1]
    axial_block = axial_vel.shape[0]
    row_index = lax.axis_index("row")
    row_count = lax.axis_size("row")
    gz_count = lax.axis_size("gz")
    both = ("gz", "row")
    device_count = gz_count * row_count
    spacing = 2.0 * math.pi / NT
    own_first = row_index * radial_block
    own_cells = own_first + jnp.arange(radial_block, dtype=jnp.int32)
    radius = cell_radius(own_cells)[None, :, None]
    axial_pad = extended(axial_vel, (("gz", 0),), 1)
    flux = radial_vel * radius
    if row_count == 2:
        no_flux = jnp.zeros_like(flux[:, :1])
        radial_flux = radial_neighbour(flux, no_flux, no_flux)
    else:
        radial_flux = extended(flux, (("row", 1),), 1)
    divergence = 0.5 * (axial_pad[2:] - axial_pad[:-2])
    divergence = divergence + (radial_flux[:, 2:] - radial_flux[:, :-2]) / (2.0 * radius)
    divergence = divergence + (jnp.roll(swirl_vel, -1, 2) - jnp.roll(swirl_vel, 1, 2)) / (
        2.0 * radius * spacing
    )
    right_side = divergence - canopy_source(canopy_gore, inflow_rate)
    all_modes = jnp.arange(NT, dtype=jnp.int32)
    fourier = jnp.asarray(AZIMUTH_TABLE)
    spectrum_in = jnp.einsum("xrt,tm->mxr", right_side, fourier, precision=maximal_precision)
    modes_each = NT // device_count
    spectrum_in = spectrum_in.reshape(device_count, modes_each, axial_block, radial_block)
    resident = lax.all_to_all(spectrum_in, both, split_axis=0, concat_axis=0, tiled=True)
    resident = resident.reshape(gz_count, row_count, modes_each, axial_block, radial_block)
    mode_ids = lax.axis_index(both) * modes_each + jnp.arange(modes_each, dtype=jnp.int32)
    axial_table = jnp.asarray(AXIAL_TABLE).reshape(NX, gz_count, axial_block)
    radial_table = jnp.asarray(RADIAL_TABLE)
    axial_coefficient = jnp.einsum(
        "kgx,grmxj->mkrj", axial_table, resident, precision=maximal_precision
    ).reshape(modes_each, NX, NR)
    spectrum = jnp.einsum("sj,mkj->mks", radial_table, axial_coefficient, precision=maximal_precision)
    scaled = spectrum / denominator_of(mode_ids, jnp.arange(NR, dtype=jnp.int32))
    radial_returned = jnp.einsum("sj,mks->mkj", radial_table, scaled, precision=maximal_precision)
    radial_returned = radial_returned.reshape(modes_each, NX, row_count, radial_block)
    physical_space = jnp.einsum(
        "kgx,mkrj->grmxj", axial_table, radial_returned, precision=maximal_precision
    ).reshape(device_count, modes_each, axial_block, radial_block)
    returned = lax.all_to_all(physical_space, both, split_axis=0, concat_axis=0, tiled=True)
    returned = returned.reshape(NT, axial_block, radial_block)
    pressure = -jnp.einsum("qxr,tq->xrt", returned, fourier, precision=maximal_precision)
    padded = extended(pressure, (("gz", 0),), 1)
    if row_count == 2:
        sideways = radial_neighbour(pressure, pressure[:, :1], pressure[:, -1:])
        above = sideways[:, 2:]
        below = sideways[:, :-2]
    else:
        wide = extended(pressure, (("row", 1),), 1)
        lower_ghost = jnp.where(row_index == 0, pressure[:, :1], wide[:, :1])
        upper_ghost = jnp.where(row_index == row_count - 1, pressure[:, -1:], wide[:, -1:])
        above = jnp.concatenate([pressure[:, 1:], upper_ghost], axis=1)
        below = jnp.concatenate([lower_ghost, pressure[:, :-1]], axis=1)
    axial_out = axial_vel - 0.5 * (padded[2:] - padded[:-2])
    radial_projected_velocity = radial_vel - 0.5 * (above - below)
    swirl_out = swirl_vel - (jnp.roll(pressure, -1, 2) - jnp.roll(pressure, 1, 2)) / (
        2.0 * radius * spacing
    )
    return (axial_out, radial_projected_velocity, swirl_out)


def solution(mesh):
    placed = (
        P("gz", "row", None),
        P("gz", "row", None),
        P("gz", "row", None),
        P(),
        P("gz", "row", None),
    )
    return jax.shard_map(
        body,
        mesh=mesh,
        in_specs=placed,
        out_specs=(P("gz", "row", None), P("gz", "row", None), P("gz", "row", None)),
        check_vma=False,
    )
```

```python
import math

import numpy as np

import jax
import jax.numpy as jnp
from jax import lax
from jax.sharding import PartitionSpec as P

NX = 1024
NR = 256
NT = 256
GORES = 48


helmholtz_shift = 0.001
maximal_precision = lax.Precision.HIGHEST
forward_precision = lax.Precision.HIGH


def extended(block, sides, width):
    for axis, dim in sides:
        count = lax.axis_size(axis)
        forward = [(i, i + 1) for i in range(count - 1)]
        backward = [(target, source) for source, target in forward]
        low = lax.ppermute(
            lax.slice_in_dim(block, block.shape[dim] - width, None, axis=dim), axis, forward
        )
        high = lax.ppermute(lax.slice_in_dim(block, 0, width, axis=dim), axis, backward)
        block = jnp.concatenate([low, block, high], axis=dim)
    return block


def radial_neighbour(block, ghost_low, ghost_high):
    row_index = lax.axis_index("row")
    send = jnp.where(row_index == 0, block[:, -1:], block[:, :1])
    received = lax.ppermute(send, "row", [(0, 1), (1, 0)])
    low = jnp.where(row_index == 0, ghost_low, received)
    high = jnp.where(row_index == 0, received, ghost_high)
    return jnp.concatenate([low, block, high], axis=1)


def azimuth_basis(extent, mode_ids):
    positions = jnp.arange(extent, dtype=jnp.int32)
    half_way = extent // 2
    frequency = jnp.where(mode_ids <= half_way, mode_ids, mode_ids - half_way)
    phases = positions[:, None] * frequency[None, :] % extent
    angles = phases.astype(jnp.float32) * (2.0 * math.pi / extent)
    weights = jnp.where(
        (mode_ids == 0) | (mode_ids == half_way), math.sqrt(1.0 / extent), math.sqrt(2.0 / extent)
    ).astype(jnp.float32)
    return (
        jnp.where((mode_ids > half_way)[None, :], jnp.sin(angles), jnp.cos(angles))
        * weights[None, :]
    )


def azimuth_eigen(mode_ids):
    half_way = NT // 2
    frequency = jnp.where(mode_ids <= half_way, mode_ids, mode_ids - half_way)
    angles = frequency.astype(jnp.float32) * (2.0 * math.pi / NT)
    arc_step = 0.75 * NR * 2.0 * math.pi / NT
    return (2.0 - 2.0 * jnp.cos(angles)) / (arc_step * arc_step)


def axial_basis(extent):
    indices = jnp.arange(extent, dtype=jnp.int32) + 1
    phases = indices[:, None] * indices[None, :] % (2 * (extent + 1))
    angles = phases.astype(jnp.float32) * (math.pi / (extent + 1))
    return jnp.sin(angles) * math.sqrt(2.0 / (extent + 1))


def axial_eigen(extent):
    indices = jnp.arange(extent, dtype=jnp.int32) + 1
    return 2.0 - 2.0 * jnp.cos(indices.astype(jnp.float32) * (math.pi / (extent + 1)))


def radial_basis(extent):
    mode_ids = jnp.arange(extent, dtype=jnp.int32)[:, None]
    cell_ids = jnp.arange(extent, dtype=jnp.int32)[None, :]
    phases = mode_ids * (2 * cell_ids + 1) % (4 * extent)
    angles = phases.astype(jnp.float32) * (math.pi / (2 * extent))
    weights = jnp.where(mode_ids == 0, math.sqrt(1.0 / extent), math.sqrt(2.0 / extent)).astype(
        jnp.float32
    )
    return jnp.cos(angles) * weights


def radial_eigen(mode_ids):
    return 2.0 - 2.0 * jnp.cos(mode_ids.astype(jnp.float32) * (math.pi / NR))


def cell_radius(cell_ids):
    return cell_ids.astype(jnp.float32) + (0.25 * NR + 0.5)


def fixed_azimuth_basis():
    positions = np.arange(NT)[:, None]
    modes = np.arange(NT)[None, :]
    frequency = np.where(modes <= NT // 2, modes, modes - NT // 2)
    angles = (positions * frequency % NT) * (2.0 * math.pi / NT)
    weights = np.where((modes == 0) | (modes == NT // 2), math.sqrt(1.0 / NT), math.sqrt(2.0 / NT))
    return (np.where(modes > NT // 2, np.sin(angles), np.cos(angles)) * weights).astype(np.float32)


def fixed_axial_basis():
    indices = np.arange(1, NX + 1)
    phases = indices[:, None] * indices[None, :] % (2 * (NX + 1))
    return (np.sin(phases * (math.pi / (NX + 1))) * math.sqrt(2.0 / (NX + 1))).astype(np.float32)


def fixed_radial_basis():
    modes = np.arange(NR)[:, None]
    cells = np.arange(NR)[None, :]
    angles = (modes * (2 * cells + 1) % (4 * NR)) * (math.pi / (2 * NR))
    weights = np.where(modes == 0, math.sqrt(1.0 / NR), math.sqrt(2.0 / NR))
    return (np.cos(angles) * weights).astype(np.float32)


AZIMUTH_TABLE = fixed_azimuth_basis()
AXIAL_TABLE = fixed_axial_basis()
RADIAL_TABLE = fixed_radial_basis()


def denominator_of(mode_ids, radial_ids):
    total = azimuth_eigen(mode_ids)[:, None, None] + axial_eigen(NX)[None, :, None]
    return total + radial_eigen(radial_ids)[None, None, :] + helmholtz_shift


def canopy_source(gore_map, rate_table):
    gore_ids = jnp.arange(rate_table.shape[0], dtype=jnp.int32)
    column_gore = jnp.arange(NT, dtype=jnp.int32) * GORES // NT
    matches = column_gore[:, None] == gore_ids[None, :]
    column_rate = jnp.sum(jnp.where(matches, rate_table[None, :], 0.0), axis=1)
    return jnp.where(gore_map < GORES, column_rate[None, None, :], 0.0)


def body(axial_vel, radial_vel, swirl_vel, inflow_rate, canopy_gore):
    radial_block = axial_vel.shape[1]
    axial_block = axial_vel.shape[0]
    row_index = lax.axis_index("row")
    row_count = lax.axis_size("row")
    gz_count = lax.axis_size("gz")
    both = ("gz", "row")
    device_count = gz_count * row_count
    spacing = 2.0 * math.pi / NT
    own_first = row_index * radial_block
    own_cells = own_first + jnp.arange(radial_block, dtype=jnp.int32)
    radius = cell_radius(own_cells)[None, :, None]
    axial_pad = extended(axial_vel, (("gz", 0),), 1)
    flux = radial_vel * radius
    if row_count == 2:
        no_flux = jnp.zeros_like(flux[:, :1])
        radial_flux = radial_neighbour(flux, no_flux, no_flux)
    else:
        radial_flux = extended(flux, (("row", 1),), 1)
    divergence = 0.5 * (axial_pad[2:] - axial_pad[:-2])
    divergence = divergence + (radial_flux[:, 2:] - radial_flux[:, :-2]) / (2.0 * radius)
    divergence = divergence + (jnp.roll(swirl_vel, -1, 2) - jnp.roll(swirl_vel, 1, 2)) / (
        2.0 * radius * spacing
    )
    right_side = divergence - canopy_source(canopy_gore, inflow_rate)
    all_modes = jnp.arange(NT, dtype=jnp.int32)
    fourier = jnp.asarray(AZIMUTH_TABLE)
    spectrum_in = jnp.einsum("xrt,tm->mxr", right_side, fourier, precision=forward_precision)
    modes_each = NT // device_count
    spectrum_in = spectrum_in.reshape(device_count, modes_each, axial_block, radial_block)
    resident = lax.all_to_all(spectrum_in, both, split_axis=0, concat_axis=0, tiled=True)
    resident = resident.reshape(gz_count, row_count, modes_each, axial_block, radial_block)
    mode_ids = lax.axis_index(both) * modes_each + jnp.arange(modes_each, dtype=jnp.int32)
    axial_table = jnp.asarray(AXIAL_TABLE).reshape(NX, gz_count, axial_block)
    radial_table = jnp.asarray(RADIAL_TABLE)
    axial_coefficient = jnp.einsum(
        "kgx,grmxj->mkrj", axial_table, resident, precision=forward_precision
    ).reshape(modes_each, NX, NR)
    spectrum = jnp.einsum("sj,mkj->mks", radial_table, axial_coefficient, precision=forward_precision)
    scaled = spectrum / denominator_of(mode_ids, jnp.arange(NR, dtype=jnp.int32))
    radial_returned = jnp.einsum("sj,mks->mkj", radial_table, scaled, precision=maximal_precision)
    radial_returned = radial_returned.reshape(modes_each, NX, row_count, radial_block)
    physical_space = jnp.einsum(
        "kgx,mkrj->grmxj", axial_table, radial_returned, precision=maximal_precision
    ).reshape(device_count, modes_each, axial_block, radial_block)
    returned = lax.all_to_all(physical_space, both, split_axis=0, concat_axis=0, tiled=True)
    returned = returned.reshape(NT, axial_block, radial_block)
    pressure = -jnp.einsum("qxr,tq->xrt", returned, fourier, precision=maximal_precision)
    padded = extended(pressure, (("gz", 0),), 1)
    if row_count == 2:
        sideways = radial_neighbour(pressure, pressure[:, :1], pressure[:, -1:])
        above = sideways[:, 2:]
        below = sideways[:, :-2]
    else:
        wide = extended(pressure, (("row", 1),), 1)
        lower_ghost = jnp.where(row_index == 0, pressure[:, :1], wide[:, :1])
        upper_ghost = jnp.where(row_index == row_count - 1, pressure[:, -1:], wide[:, -1:])
        above = jnp.concatenate([pressure[:, 1:], upper_ghost], axis=1)
        below = jnp.concatenate([lower_ghost, pressure[:, :-1]], axis=1)
    axial_out = axial_vel - 0.5 * (padded[2:] - padded[:-2])
    radial_projected_velocity = radial_vel - 0.5 * (above - below)
    swirl_out = swirl_vel - (jnp.roll(pressure, -1, 2) - jnp.roll(pressure, 1, 2)) / (
        2.0 * radius * spacing
    )
    return (axial_out, radial_projected_velocity, swirl_out)


def solution(mesh):
    placed = (
        P("gz", "row", None),
        P("gz", "row", None),
        P("gz", "row", None),
        P(),
        P("gz", "row", None),
    )
    return jax.shard_map(
        body,
        mesh=mesh,
        in_specs=placed,
        out_specs=(P("gz", "row", None), P("gz", "row", None), P("gz", "row", None)),
        check_vma=False,
    )
```

```python
import math

import numpy as np

import jax
import jax.numpy as jnp
from jax import lax
from jax.sharding import PartitionSpec as P

NX = 1024
NR = 256
NT = 256
GORES = 48


helmholtz_shift = 0.001
maximal_precision = lax.Precision.HIGHEST
forward_precision = lax.Precision.HIGH


def extended(block, sides, width):
    for axis, dim in sides:
        count = lax.axis_size(axis)
        forward = [(i, i + 1) for i in range(count - 1)]
        backward = [(target, source) for source, target in forward]
        low = lax.ppermute(
            lax.slice_in_dim(block, block.shape[dim] - width, None, axis=dim), axis, forward
        )
        high = lax.ppermute(lax.slice_in_dim(block, 0, width, axis=dim), axis, backward)
        block = jnp.concatenate([low, block, high], axis=dim)
    return block


def radial_neighbour(block, ghost_low, ghost_high):
    row_index = lax.axis_index("row")
    send = jnp.where(row_index == 0, block[:, -1:], block[:, :1])
    received = lax.ppermute(send, "row", [(0, 1), (1, 0)])
    low = jnp.where(row_index == 0, ghost_low, received)
    high = jnp.where(row_index == 0, received, ghost_high)
    return jnp.concatenate([low, block, high], axis=1)


def azimuth_basis(extent, mode_ids):
    positions = jnp.arange(extent, dtype=jnp.int32)
    half_way = extent // 2
    frequency = jnp.where(mode_ids <= half_way, mode_ids, mode_ids - half_way)
    phases = positions[:, None] * frequency[None, :] % extent
    angles = phases.astype(jnp.float32) * (2.0 * math.pi / extent)
    weights = jnp.where(
        (mode_ids == 0) | (mode_ids == half_way), math.sqrt(1.0 / extent), math.sqrt(2.0 / extent)
    ).astype(jnp.float32)
    return (
        jnp.where((mode_ids > half_way)[None, :], jnp.sin(angles), jnp.cos(angles))
        * weights[None, :]
    )


def azimuth_eigen(mode_ids):
    half_way = NT // 2
    frequency = jnp.where(mode_ids <= half_way, mode_ids, mode_ids - half_way)
    angles = frequency.astype(jnp.float32) * (2.0 * math.pi / NT)
    arc_step = 0.75 * NR * 2.0 * math.pi / NT
    return (2.0 - 2.0 * jnp.cos(angles)) / (arc_step * arc_step)


def axial_basis(extent):
    indices = jnp.arange(extent, dtype=jnp.int32) + 1
    phases = indices[:, None] * indices[None, :] % (2 * (extent + 1))
    angles = phases.astype(jnp.float32) * (math.pi / (extent + 1))
    return jnp.sin(angles) * math.sqrt(2.0 / (extent + 1))


def axial_eigen(extent):
    indices = jnp.arange(extent, dtype=jnp.int32) + 1
    return 2.0 - 2.0 * jnp.cos(indices.astype(jnp.float32) * (math.pi / (extent + 1)))


def radial_basis(extent):
    mode_ids = jnp.arange(extent, dtype=jnp.int32)[:, None]
    cell_ids = jnp.arange(extent, dtype=jnp.int32)[None, :]
    phases = mode_ids * (2 * cell_ids + 1) % (4 * extent)
    angles = phases.astype(jnp.float32) * (math.pi / (2 * extent))
    weights = jnp.where(mode_ids == 0, math.sqrt(1.0 / extent), math.sqrt(2.0 / extent)).astype(
        jnp.float32
    )
    return jnp.cos(angles) * weights


def radial_eigen(mode_ids):
    return 2.0 - 2.0 * jnp.cos(mode_ids.astype(jnp.float32) * (math.pi / NR))


def cell_radius(cell_ids):
    return cell_ids.astype(jnp.float32) + (0.25 * NR + 0.5)


def fixed_azimuth_basis():
    positions = np.arange(NT)[:, None]
    modes = np.arange(NT)[None, :]
    frequency = np.where(modes <= NT // 2, modes, modes - NT // 2)
    angles = (positions * frequency % NT) * (2.0 * math.pi / NT)
    weights = np.where((modes == 0) | (modes == NT // 2), math.sqrt(1.0 / NT), math.sqrt(2.0 / NT))
    return (np.where(modes > NT // 2, np.sin(angles), np.cos(angles)) * weights).astype(np.float32)


def fixed_axial_basis():
    indices = np.arange(1, NX + 1)
    phases = indices[:, None] * indices[None, :] % (2 * (NX + 1))
    return (np.sin(phases * (math.pi / (NX + 1))) * math.sqrt(2.0 / (NX + 1))).astype(np.float32)


def fixed_radial_basis():
    modes = np.arange(NR)[:, None]
    cells = np.arange(NR)[None, :]
    angles = (modes * (2 * cells + 1) % (4 * NR)) * (math.pi / (2 * NR))
    weights = np.where(modes == 0, math.sqrt(1.0 / NR), math.sqrt(2.0 / NR))
    return (np.cos(angles) * weights).astype(np.float32)


AZIMUTH_TABLE = fixed_azimuth_basis()
AXIAL_TABLE = fixed_axial_basis()
RADIAL_TABLE = fixed_radial_basis()


def denominator_of(mode_ids, radial_ids):
    total = azimuth_eigen(mode_ids)[:, None, None] + axial_eigen(NX)[None, :, None]
    return total + radial_eigen(radial_ids)[None, None, :] + helmholtz_shift


def canopy_source(gore_map, rate_table):
    gore_ids = jnp.arange(rate_table.shape[0], dtype=jnp.int32)
    column_gore = jnp.arange(NT, dtype=jnp.int32) * GORES // NT
    matches = column_gore[:, None] == gore_ids[None, :]
    column_rate = jnp.sum(jnp.where(matches, rate_table[None, :], 0.0), axis=1)
    return jnp.where(gore_map < GORES, column_rate[None, None, :], 0.0)


def body(axial_vel, radial_vel, swirl_vel, inflow_rate, canopy_gore):
    radial_block = axial_vel.shape[1]
    axial_block = axial_vel.shape[0]
    row_index = lax.axis_index("row")
    row_count = lax.axis_size("row")
    gz_count = lax.axis_size("gz")
    both = ("gz", "row")
    device_count = gz_count * row_count
    spacing = 2.0 * math.pi / NT
    own_first = row_index * radial_block
    own_cells = own_first + jnp.arange(radial_block, dtype=jnp.int32)
    radius = cell_radius(own_cells)[None, :, None]
    axial_pad = extended(axial_vel, (("gz", 0),), 1)
    flux = radial_vel * radius
    if row_count == 2:
        edge_radius = jnp.where(row_index == 0, radius[:, -1:], radius[:, :1])
        edge_vel = jnp.where(row_index == 0, radial_vel[:, -1:], radial_vel[:, :1])
        received = lax.ppermute(edge_vel * edge_radius, "row", [(0, 1), (1, 0)])
        no_flux = jnp.zeros_like(received)
        low = jnp.where(row_index == 0, no_flux, received)
        high = jnp.where(row_index == 0, received, no_flux)
        radial_flux = jnp.concatenate([low, flux, high], axis=1)
    else:
        radial_flux = extended(flux, (("row", 1),), 1)
    divergence = 0.5 * (axial_pad[2:] - axial_pad[:-2])
    divergence = divergence + (radial_flux[:, 2:] - radial_flux[:, :-2]) / (2.0 * radius)
    divergence = divergence + (jnp.roll(swirl_vel, -1, 2) - jnp.roll(swirl_vel, 1, 2)) / (
        2.0 * radius * spacing
    )
    right_side = divergence - canopy_source(canopy_gore, inflow_rate)
    all_modes = jnp.arange(NT, dtype=jnp.int32)
    fourier = jnp.asarray(AZIMUTH_TABLE)
    spectrum_in = jnp.einsum("xrt,tm->mxr", right_side, fourier, precision=forward_precision)
    modes_each = NT // device_count
    spectrum_in = spectrum_in.reshape(device_count, modes_each, axial_block, radial_block)
    resident = lax.all_to_all(spectrum_in, both, split_axis=0, concat_axis=0, tiled=True)
    resident = resident.reshape(gz_count, row_count, modes_each, axial_block, radial_block)
    mode_ids = lax.axis_index(both) * modes_each + jnp.arange(modes_each, dtype=jnp.int32)
    axial_table = jnp.asarray(AXIAL_TABLE).reshape(NX, gz_count, axial_block)
    radial_table = jnp.asarray(RADIAL_TABLE)
    axial_coefficient = jnp.einsum(
        "kgx,grmxj->mkrj", axial_table, resident, precision=forward_precision
    ).reshape(modes_each, NX, NR)
    spectrum = jnp.einsum("sj,mkj->mks", radial_table, axial_coefficient, precision=forward_precision)
    scaled = spectrum / denominator_of(mode_ids, jnp.arange(NR, dtype=jnp.int32))
    radial_returned = jnp.einsum("sj,mks->mkj", radial_table, scaled, precision=maximal_precision)
    radial_returned = radial_returned.reshape(modes_each, NX, row_count, radial_block)
    physical_space = jnp.einsum(
        "kgx,mkrj->grmxj", axial_table, radial_returned, precision=maximal_precision
    ).reshape(device_count, modes_each, axial_block, radial_block)
    returned = lax.all_to_all(physical_space, both, split_axis=0, concat_axis=0, tiled=True)
    returned = returned.reshape(NT, axial_block, radial_block)
    pressure = -jnp.einsum("qxr,tq->xrt", returned, fourier, precision=maximal_precision)
    padded = extended(pressure, (("gz", 0),), 1)
    if row_count == 2:
        sideways = radial_neighbour(pressure, pressure[:, :1], pressure[:, -1:])
        above = sideways[:, 2:]
        below = sideways[:, :-2]
    else:
        wide = extended(pressure, (("row", 1),), 1)
        lower_ghost = jnp.where(row_index == 0, pressure[:, :1], wide[:, :1])
        upper_ghost = jnp.where(row_index == row_count - 1, pressure[:, -1:], wide[:, -1:])
        above = jnp.concatenate([pressure[:, 1:], upper_ghost], axis=1)
        below = jnp.concatenate([lower_ghost, pressure[:, :-1]], axis=1)
    axial_out = axial_vel - 0.5 * (padded[2:] - padded[:-2])
    radial_projected_velocity = radial_vel - 0.5 * (above - below)
    swirl_out = swirl_vel - (jnp.roll(pressure, -1, 2) - jnp.roll(pressure, 1, 2)) / (
        2.0 * radius * spacing
    )
    return (axial_out, radial_projected_velocity, swirl_out)


def solution(mesh):
    placed = (
        P("gz", "row", None),
        P("gz", "row", None),
        P("gz", "row", None),
        P(),
        P("gz", "row", None),
    )
    return jax.shard_map(
        body,
        mesh=mesh,
        in_specs=placed,
        out_specs=(P("gz", "row", None), P("gz", "row", None), P("gz", "row", None)),
        check_vma=False,
    )
```

```python
import math

import numpy as np

import jax
import jax.numpy as jnp
from jax import lax
from jax.sharding import PartitionSpec as P

NX = 1024
NR = 256
NT = 256
GORES = 48


helmholtz_shift = 0.001
maximal_precision = lax.Precision.HIGHEST
forward_precision = lax.Precision.HIGH


def extended(block, sides, width):
    for axis, dim in sides:
        count = lax.axis_size(axis)
        forward = [(i, i + 1) for i in range(count - 1)]
        backward = [(target, source) for source, target in forward]
        low = lax.ppermute(
            lax.slice_in_dim(block, block.shape[dim] - width, None, axis=dim), axis, forward
        )
        high = lax.ppermute(lax.slice_in_dim(block, 0, width, axis=dim), axis, backward)
        block = jnp.concatenate([low, block, high], axis=dim)
    return block


def radial_neighbour(block, ghost_low, ghost_high):
    row_index = lax.axis_index("row")
    send = jnp.where(row_index == 0, block[:, -1:], block[:, :1])
    received = lax.ppermute(send, "row", [(0, 1), (1, 0)])
    low = jnp.where(row_index == 0, ghost_low, received)
    high = jnp.where(row_index == 0, received, ghost_high)
    return jnp.concatenate([low, block, high], axis=1)


def azimuth_basis(extent, mode_ids):
    positions = jnp.arange(extent, dtype=jnp.int32)
    half_way = extent // 2
    frequency = jnp.where(mode_ids <= half_way, mode_ids, mode_ids - half_way)
    phases = positions[:, None] * frequency[None, :] % extent
    angles = phases.astype(jnp.float32) * (2.0 * math.pi / extent)
    weights = jnp.where(
        (mode_ids == 0) | (mode_ids == half_way), math.sqrt(1.0 / extent), math.sqrt(2.0 / extent)
    ).astype(jnp.float32)
    return (
        jnp.where((mode_ids > half_way)[None, :], jnp.sin(angles), jnp.cos(angles))
        * weights[None, :]
    )


def azimuth_eigen(mode_ids):
    half_way = NT // 2
    frequency = jnp.where(mode_ids <= half_way, mode_ids, mode_ids - half_way)
    angles = frequency.astype(jnp.float32) * (2.0 * math.pi / NT)
    arc_step = 0.75 * NR * 2.0 * math.pi / NT
    return (2.0 - 2.0 * jnp.cos(angles)) / (arc_step * arc_step)


def axial_basis(extent):
    indices = jnp.arange(extent, dtype=jnp.int32) + 1
    phases = indices[:, None] * indices[None, :] % (2 * (extent + 1))
    angles = phases.astype(jnp.float32) * (math.pi / (extent + 1))
    return jnp.sin(angles) * math.sqrt(2.0 / (extent + 1))


def axial_eigen(extent):
    indices = jnp.arange(extent, dtype=jnp.int32) + 1
    return 2.0 - 2.0 * jnp.cos(indices.astype(jnp.float32) * (math.pi / (extent + 1)))


def radial_basis(extent):
    mode_ids = jnp.arange(extent, dtype=jnp.int32)[:, None]
    cell_ids = jnp.arange(extent, dtype=jnp.int32)[None, :]
    phases = mode_ids * (2 * cell_ids + 1) % (4 * extent)
    angles = phases.astype(jnp.float32) * (math.pi / (2 * extent))
    weights = jnp.where(mode_ids == 0, math.sqrt(1.0 / extent), math.sqrt(2.0 / extent)).astype(
        jnp.float32
    )
    return jnp.cos(angles) * weights


def radial_eigen(mode_ids):
    return 2.0 - 2.0 * jnp.cos(mode_ids.astype(jnp.float32) * (math.pi / NR))


def cell_radius(cell_ids):
    return cell_ids.astype(jnp.float32) + (0.25 * NR + 0.5)


def fixed_azimuth_basis():
    positions = np.arange(NT)[:, None]
    modes = np.arange(NT)[None, :]
    frequency = np.where(modes <= NT // 2, modes, modes - NT // 2)
    angles = (positions * frequency % NT) * (2.0 * math.pi / NT)
    weights = np.where((modes == 0) | (modes == NT // 2), math.sqrt(1.0 / NT), math.sqrt(2.0 / NT))
    return (np.where(modes > NT // 2, np.sin(angles), np.cos(angles)) * weights).astype(np.float32)


def fixed_axial_basis():
    indices = np.arange(1, NX + 1)
    phases = indices[:, None] * indices[None, :] % (2 * (NX + 1))
    return (np.sin(phases * (math.pi / (NX + 1))) * math.sqrt(2.0 / (NX + 1))).astype(np.float32)


def fixed_radial_basis():
    modes = np.arange(NR)[:, None]
    cells = np.arange(NR)[None, :]
    angles = (modes * (2 * cells + 1) % (4 * NR)) * (math.pi / (2 * NR))
    weights = np.where(modes == 0, math.sqrt(1.0 / NR), math.sqrt(2.0 / NR))
    return (np.cos(angles) * weights).astype(np.float32)


AZIMUTH_TABLE = fixed_azimuth_basis()
AXIAL_TABLE = fixed_axial_basis()
RADIAL_TABLE = fixed_radial_basis()


def denominator_of(mode_ids, radial_ids):
    total = azimuth_eigen(mode_ids)[:, None, None] + axial_eigen(NX)[None, :, None]
    return total + radial_eigen(radial_ids)[None, None, :] + helmholtz_shift


def canopy_source(gore_map, rate_table):
    gore_ids = jnp.arange(rate_table.shape[0], dtype=jnp.int32)
    column_gore = jnp.arange(NT, dtype=jnp.int32) * GORES // NT
    matches = column_gore[:, None] == gore_ids[None, :]
    column_rate = jnp.sum(jnp.where(matches, rate_table[None, :], 0.0), axis=1)
    return jnp.where(gore_map < GORES, column_rate[None, None, :], 0.0)


def body(axial_vel, radial_vel, swirl_vel, inflow_rate, canopy_gore):
    radial_block = axial_vel.shape[1]
    axial_block = axial_vel.shape[0]
    row_index = lax.axis_index("row")
    row_count = lax.axis_size("row")
    gz_count = lax.axis_size("gz")
    both = ("gz", "row")
    device_count = gz_count * row_count
    spacing = 2.0 * math.pi / NT
    own_first = row_index * radial_block
    own_cells = own_first + jnp.arange(radial_block, dtype=jnp.int32)
    radius = cell_radius(own_cells)[None, :, None]
    axial_pad = jnp.pad(axial_vel, ((1, 1), (0, 0), (0, 0)))
    flux = radial_vel * radius
    if row_count == 2:
        no_flux = jnp.zeros_like(flux[:, :1])
        radial_flux = radial_neighbour(flux, no_flux, no_flux)
    else:
        radial_flux = extended(flux, (("row", 1),), 1)
    divergence = 0.5 * (axial_pad[2:] - axial_pad[:-2])
    divergence = divergence + (radial_flux[:, 2:] - radial_flux[:, :-2]) / (2.0 * radius)
    divergence = divergence + (jnp.roll(swirl_vel, -1, 2) - jnp.roll(swirl_vel, 1, 2)) / (
        2.0 * radius * spacing
    )
    right_side = divergence - canopy_source(canopy_gore, inflow_rate)
    all_modes = jnp.arange(NT, dtype=jnp.int32)
    fourier = jnp.asarray(AZIMUTH_TABLE)
    planes = jnp.concatenate([right_side, axial_vel[:1], axial_vel[-1:]], axis=0)
    spectrum_in = jnp.einsum("xrt,tm->mxr", planes, fourier, precision=forward_precision)
    modes_each = NT // device_count
    spectrum_in = spectrum_in.reshape(device_count, modes_each, axial_block + 2, radial_block)
    resident = lax.all_to_all(spectrum_in, both, split_axis=0, concat_axis=0, tiled=True)
    resident = resident.reshape(gz_count, row_count, modes_each, axial_block + 2, radial_block)
    first_hat = resident[:, :, :, axial_block]
    last_hat = resident[:, :, :, axial_block + 1]
    next_first = jnp.concatenate([first_hat[1:], jnp.zeros_like(first_hat[:1])], axis=0)
    prev_last = jnp.concatenate([jnp.zeros_like(last_hat[:1]), last_hat[:-1]], axis=0)
    resident = resident[:, :, :, :axial_block]
    resident = resident.at[:, :, :, axial_block - 1].add(0.5 * next_first)
    resident = resident.at[:, :, :, 0].add(-0.5 * prev_last)
    mode_ids = lax.axis_index(both) * modes_each + jnp.arange(modes_each, dtype=jnp.int32)
    axial_table = jnp.asarray(AXIAL_TABLE).reshape(NX, gz_count, axial_block)
    radial_table = jnp.asarray(RADIAL_TABLE)
    axial_coefficient = jnp.einsum(
        "kgx,grmxj->mkrj", axial_table, resident, precision=forward_precision
    ).reshape(modes_each, NX, NR)
    spectrum = jnp.einsum("sj,mkj->mks", radial_table, axial_coefficient, precision=forward_precision)
    scaled = spectrum / denominator_of(mode_ids, jnp.arange(NR, dtype=jnp.int32))
    radial_returned = jnp.einsum("sj,mks->mkj", radial_table, scaled, precision=maximal_precision)
    radial_returned = radial_returned.reshape(modes_each, NX, row_count, radial_block)
    physical_space = jnp.einsum(
        "kgx,mkrj->grmxj", axial_table, radial_returned, precision=maximal_precision
    )
    first_p = physical_space[:, :, :, :1]
    last_p = physical_space[:, :, :, -1:]
    ghost_low = jnp.concatenate([jnp.zeros_like(last_p[:1]), last_p[:-1]], axis=0)
    ghost_high = jnp.concatenate([first_p[1:], jnp.zeros_like(first_p[:1])], axis=0)
    windows = jnp.concatenate([physical_space, ghost_low, ghost_high], axis=3)
    windows = windows.reshape(device_count, modes_each, axial_block + 2, radial_block)
    returned = lax.all_to_all(windows, both, split_axis=0, concat_axis=0, tiled=True)
    returned = returned.reshape(NT, axial_block + 2, radial_block)
    extended_p = -jnp.einsum("qxr,tq->xrt", returned, fourier, precision=maximal_precision)
    pressure = extended_p[:axial_block]
    padded = jnp.concatenate(
        [extended_p[axial_block : axial_block + 1], pressure, extended_p[axial_block + 1 :]], axis=0
    )
    if row_count == 2:
        sideways = radial_neighbour(pressure, pressure[:, :1], pressure[:, -1:])
        above = sideways[:, 2:]
        below = sideways[:, :-2]
    else:
        wide = extended(pressure, (("row", 1),), 1)
        lower_ghost = jnp.where(row_index == 0, pressure[:, :1], wide[:, :1])
        upper_ghost = jnp.where(row_index == row_count - 1, pressure[:, -1:], wide[:, -1:])
        above = jnp.concatenate([pressure[:, 1:], upper_ghost], axis=1)
        below = jnp.concatenate([lower_ghost, pressure[:, :-1]], axis=1)
    axial_out = axial_vel - 0.5 * (padded[2:] - padded[:-2])
    radial_projected_velocity = radial_vel - 0.5 * (above - below)
    swirl_out = swirl_vel - (jnp.roll(pressure, -1, 2) - jnp.roll(pressure, 1, 2)) / (
        2.0 * radius * spacing
    )
    return (axial_out, radial_projected_velocity, swirl_out)


def solution(mesh):
    placed = (
        P("gz", "row", None),
        P("gz", "row", None),
        P("gz", "row", None),
        P(),
        P("gz", "row", None),
    )
    return jax.shard_map(
        body,
        mesh=mesh,
        in_specs=placed,
        out_specs=(P("gz", "row", None), P("gz", "row", None), P("gz", "row", None)),
        check_vma=False,
    )
```

```python
import math

import numpy as np

import jax
import jax.numpy as jnp
from jax import lax
from jax.sharding import PartitionSpec as P

NX = 1024
NR = 256
NT = 256
GORES = 48


helmholtz_shift = 0.001
maximal_precision = lax.Precision.HIGHEST
forward_precision = lax.Precision.HIGH


def extended(block, sides, width):
    for axis, dim in sides:
        count = lax.axis_size(axis)
        forward = [(i, i + 1) for i in range(count - 1)]
        backward = [(target, source) for source, target in forward]
        low = lax.ppermute(
            lax.slice_in_dim(block, block.shape[dim] - width, None, axis=dim), axis, forward
        )
        high = lax.ppermute(lax.slice_in_dim(block, 0, width, axis=dim), axis, backward)
        block = jnp.concatenate([low, block, high], axis=dim)
    return block


def radial_neighbour(block, ghost_low, ghost_high):
    row_index = lax.axis_index("row")
    send = jnp.where(row_index == 0, block[:, -1:], block[:, :1])
    received = lax.ppermute(send, "row", [(0, 1), (1, 0)])
    low = jnp.where(row_index == 0, ghost_low, received)
    high = jnp.where(row_index == 0, received, ghost_high)
    return jnp.concatenate([low, block, high], axis=1)


def azimuth_basis(extent, mode_ids):
    positions = jnp.arange(extent, dtype=jnp.int32)
    half_way = extent // 2
    frequency = jnp.where(mode_ids <= half_way, mode_ids, mode_ids - half_way)
    phases = positions[:, None] * frequency[None, :] % extent
    angles = phases.astype(jnp.float32) * (2.0 * math.pi / extent)
    weights = jnp.where(
        (mode_ids == 0) | (mode_ids == half_way), math.sqrt(1.0 / extent), math.sqrt(2.0 / extent)
    ).astype(jnp.float32)
    return (
        jnp.where((mode_ids > half_way)[None, :], jnp.sin(angles), jnp.cos(angles))
        * weights[None, :]
    )


def azimuth_eigen(mode_ids):
    half_way = NT // 2
    frequency = jnp.where(mode_ids <= half_way, mode_ids, mode_ids - half_way)
    angles = frequency.astype(jnp.float32) * (2.0 * math.pi / NT)
    arc_step = 0.75 * NR * 2.0 * math.pi / NT
    return (2.0 - 2.0 * jnp.cos(angles)) / (arc_step * arc_step)


def axial_basis(extent):
    indices = jnp.arange(extent, dtype=jnp.int32) + 1
    phases = indices[:, None] * indices[None, :] % (2 * (extent + 1))
    angles = phases.astype(jnp.float32) * (math.pi / (extent + 1))
    return jnp.sin(angles) * math.sqrt(2.0 / (extent + 1))


def axial_eigen(extent):
    indices = jnp.arange(extent, dtype=jnp.int32) + 1
    return 2.0 - 2.0 * jnp.cos(indices.astype(jnp.float32) * (math.pi / (extent + 1)))


def radial_basis(extent):
    mode_ids = jnp.arange(extent, dtype=jnp.int32)[:, None]
    cell_ids = jnp.arange(extent, dtype=jnp.int32)[None, :]
    phases = mode_ids * (2 * cell_ids + 1) % (4 * extent)
    angles = phases.astype(jnp.float32) * (math.pi / (2 * extent))
    weights = jnp.where(mode_ids == 0, math.sqrt(1.0 / extent), math.sqrt(2.0 / extent)).astype(
        jnp.float32
    )
    return jnp.cos(angles) * weights


def radial_eigen(mode_ids):
    return 2.0 - 2.0 * jnp.cos(mode_ids.astype(jnp.float32) * (math.pi / NR))


def cell_radius(cell_ids):
    return cell_ids.astype(jnp.float32) + (0.25 * NR + 0.5)


def fixed_azimuth_basis():
    positions = np.arange(NT)[:, None]
    modes = np.arange(NT)[None, :]
    frequency = np.where(modes <= NT // 2, modes, modes - NT // 2)
    angles = (positions * frequency % NT) * (2.0 * math.pi / NT)
    weights = np.where((modes == 0) | (modes == NT // 2), math.sqrt(1.0 / NT), math.sqrt(2.0 / NT))
    return (np.where(modes > NT // 2, np.sin(angles), np.cos(angles)) * weights).astype(np.float32)


def fixed_axial_basis():
    indices = np.arange(1, NX + 1)
    phases = indices[:, None] * indices[None, :] % (2 * (NX + 1))
    return (np.sin(phases * (math.pi / (NX + 1))) * math.sqrt(2.0 / (NX + 1))).astype(np.float32)


def fixed_radial_basis():
    modes = np.arange(NR)[:, None]
    cells = np.arange(NR)[None, :]
    angles = (modes * (2 * cells + 1) % (4 * NR)) * (math.pi / (2 * NR))
    weights = np.where(modes == 0, math.sqrt(1.0 / NR), math.sqrt(2.0 / NR))
    return (np.cos(angles) * weights).astype(np.float32)


AZIMUTH_TABLE = fixed_azimuth_basis()
AXIAL_TABLE = fixed_axial_basis()
RADIAL_TABLE = fixed_radial_basis()


def denominator_of(mode_ids, radial_ids):
    total = azimuth_eigen(mode_ids)[:, None, None] + axial_eigen(NX)[None, :, None]
    return total + radial_eigen(radial_ids)[None, None, :] + helmholtz_shift


def canopy_source(gore_map, rate_table):
    gore_ids = jnp.arange(rate_table.shape[0], dtype=jnp.int32)
    column_gore = jnp.arange(NT, dtype=jnp.int32) * GORES // NT
    matches = column_gore[:, None] == gore_ids[None, :]
    column_rate = jnp.sum(jnp.where(matches, rate_table[None, :], 0.0), axis=1)
    return jnp.where(gore_map < GORES, column_rate[None, None, :], 0.0)


def body(axial_vel, radial_vel, swirl_vel, inflow_rate, canopy_gore):
    radial_block = axial_vel.shape[1]
    axial_block = axial_vel.shape[0]
    row_index = lax.axis_index("row")
    row_count = lax.axis_size("row")
    gz_count = lax.axis_size("gz")
    both = ("gz", "row")
    device_count = gz_count * row_count
    spacing = 2.0 * math.pi / NT
    own_first = row_index * radial_block
    own_cells = own_first + jnp.arange(radial_block, dtype=jnp.int32)
    radius = cell_radius(own_cells)[None, :, None]
    axial_pad = jnp.pad(axial_vel, ((1, 1), (0, 0), (0, 0)))
    flux = radial_vel * radius
    if row_count == 2:
        no_flux = jnp.zeros_like(flux[:, :1])
        radial_flux = radial_neighbour(flux, no_flux, no_flux)
    else:
        radial_flux = extended(flux, (("row", 1),), 1)
    divergence = 0.5 * (axial_pad[2:] - axial_pad[:-2])
    divergence = divergence + (radial_flux[:, 2:] - radial_flux[:, :-2]) / (2.0 * radius)
    divergence = divergence + (jnp.roll(swirl_vel, -1, 2) - jnp.roll(swirl_vel, 1, 2)) / (
        2.0 * radius * spacing
    )
    right_side = divergence - canopy_source(canopy_gore, inflow_rate)
    all_modes = jnp.arange(NT, dtype=jnp.int32)
    fourier = jnp.asarray(AZIMUTH_TABLE)
    planes = jnp.concatenate([right_side, axial_vel[:1], axial_vel[-1:]], axis=0)
    modes_each = NT // device_count
    spectrum_in = jnp.einsum(
        "xrt,tds->dxsr",
        planes,
        fourier.reshape(NT, device_count, modes_each),
        precision=forward_precision,
    ).reshape(device_count, axial_block + 2, modes_each, radial_block).transpose(0, 2, 1, 3)
    resident = lax.all_to_all(spectrum_in, both, split_axis=0, concat_axis=0, tiled=True)
    resident = resident.reshape(gz_count, row_count, modes_each, axial_block + 2, radial_block)
    first_hat = resident[:, :, :, axial_block]
    last_hat = resident[:, :, :, axial_block + 1]
    next_first = jnp.concatenate([first_hat[1:], jnp.zeros_like(first_hat[:1])], axis=0)
    prev_last = jnp.concatenate([jnp.zeros_like(last_hat[:1]), last_hat[:-1]], axis=0)
    resident = resident[:, :, :, :axial_block]
    resident = resident.at[:, :, :, axial_block - 1].add(0.5 * next_first)
    resident = resident.at[:, :, :, 0].add(-0.5 * prev_last)
    mode_ids = lax.axis_index(both) * modes_each + jnp.arange(modes_each, dtype=jnp.int32)
    axial_table = jnp.asarray(AXIAL_TABLE).reshape(NX, gz_count, axial_block)
    radial_table = jnp.asarray(RADIAL_TABLE)
    axial_coefficient = jnp.einsum(
        "kgx,grmxj->mkrj", axial_table, resident, precision=forward_precision
    ).reshape(modes_each, NX, NR)
    spectrum = jnp.einsum("sj,mkj->mks", radial_table, axial_coefficient, precision=forward_precision)
    scaled = spectrum / denominator_of(mode_ids, jnp.arange(NR, dtype=jnp.int32))
    radial_returned = jnp.einsum("sj,mks->mkj", radial_table, scaled, precision=maximal_precision)
    radial_returned = radial_returned.reshape(modes_each, NX, row_count, radial_block)
    physical_space = jnp.einsum(
        "kgx,mkrj->grmxj", axial_table, radial_returned, precision=maximal_precision
    )
    first_p = physical_space[:, :, :, :1]
    last_p = physical_space[:, :, :, -1:]
    ghost_low = jnp.concatenate([jnp.zeros_like(last_p[:1]), last_p[:-1]], axis=0)
    ghost_high = jnp.concatenate([first_p[1:], jnp.zeros_like(first_p[:1])], axis=0)
    windows = jnp.concatenate([physical_space, ghost_low, ghost_high], axis=3)
    windows = windows.reshape(device_count, modes_each, axial_block + 2, radial_block)
    returned = lax.all_to_all(windows, both, split_axis=0, concat_axis=0, tiled=True)
    returned = returned.reshape(NT, axial_block + 2, radial_block)
    extended_p = -jnp.einsum("qxr,tq->xrt", returned, fourier, precision=maximal_precision)
    pressure = extended_p[:axial_block]
    padded = jnp.concatenate(
        [extended_p[axial_block : axial_block + 1], pressure, extended_p[axial_block + 1 :]], axis=0
    )
    if row_count == 2:
        sideways = radial_neighbour(pressure, pressure[:, :1], pressure[:, -1:])
        above = sideways[:, 2:]
        below = sideways[:, :-2]
    else:
        wide = extended(pressure, (("row", 1),), 1)
        lower_ghost = jnp.where(row_index == 0, pressure[:, :1], wide[:, :1])
        upper_ghost = jnp.where(row_index == row_count - 1, pressure[:, -1:], wide[:, -1:])
        above = jnp.concatenate([pressure[:, 1:], upper_ghost], axis=1)
        below = jnp.concatenate([lower_ghost, pressure[:, :-1]], axis=1)
    axial_out = axial_vel - 0.5 * (padded[2:] - padded[:-2])
    radial_projected_velocity = radial_vel - 0.5 * (above - below)
    swirl_out = swirl_vel - (jnp.roll(pressure, -1, 2) - jnp.roll(pressure, 1, 2)) / (
        2.0 * radius * spacing
    )
    return (axial_out, radial_projected_velocity, swirl_out)


def solution(mesh):
    placed = (
        P("gz", "row", None),
        P("gz", "row", None),
        P("gz", "row", None),
        P(),
        P("gz", "row", None),
    )
    return jax.shard_map(
        body,
        mesh=mesh,
        in_specs=placed,
        out_specs=(P("gz", "row", None), P("gz", "row", None), P("gz", "row", None)),
        check_vma=False,
    )
```

```python
import math

import numpy as np

import jax
import jax.numpy as jnp
from jax import lax
from jax.sharding import PartitionSpec as P

NX = 1024
NR = 256
NT = 256
GORES = 48


helmholtz_shift = 0.001
maximal_precision = lax.Precision.HIGHEST
forward_precision = lax.Precision.HIGH


def extended(block, sides, width):
    for axis, dim in sides:
        count = lax.axis_size(axis)
        forward = [(i, i + 1) for i in range(count - 1)]
        backward = [(target, source) for source, target in forward]
        low = lax.ppermute(
            lax.slice_in_dim(block, block.shape[dim] - width, None, axis=dim), axis, forward
        )
        high = lax.ppermute(lax.slice_in_dim(block, 0, width, axis=dim), axis, backward)
        block = jnp.concatenate([low, block, high], axis=dim)
    return block


def radial_neighbour(block, ghost_low, ghost_high):
    row_index = lax.axis_index("row")
    send = jnp.where(row_index == 0, block[:, -1:], block[:, :1])
    received = lax.ppermute(send, "row", [(0, 1), (1, 0)])
    low = jnp.where(row_index == 0, ghost_low, received)
    high = jnp.where(row_index == 0, received, ghost_high)
    return jnp.concatenate([low, block, high], axis=1)


def azimuth_basis(extent, mode_ids):
    positions = jnp.arange(extent, dtype=jnp.int32)
    half_way = extent // 2
    frequency = jnp.where(mode_ids <= half_way, mode_ids, mode_ids - half_way)
    phases = positions[:, None] * frequency[None, :] % extent
    angles = phases.astype(jnp.float32) * (2.0 * math.pi / extent)
    weights = jnp.where(
        (mode_ids == 0) | (mode_ids == half_way), math.sqrt(1.0 / extent), math.sqrt(2.0 / extent)
    ).astype(jnp.float32)
    return (
        jnp.where((mode_ids > half_way)[None, :], jnp.sin(angles), jnp.cos(angles))
        * weights[None, :]
    )


def azimuth_eigen(mode_ids):
    half_way = NT // 2
    frequency = jnp.where(mode_ids <= half_way, mode_ids, mode_ids - half_way)
    angles = frequency.astype(jnp.float32) * (2.0 * math.pi / NT)
    arc_step = 0.75 * NR * 2.0 * math.pi / NT
    return (2.0 - 2.0 * jnp.cos(angles)) / (arc_step * arc_step)


def axial_basis(extent):
    indices = jnp.arange(extent, dtype=jnp.int32) + 1
    phases = indices[:, None] * indices[None, :] % (2 * (extent + 1))
    angles = phases.astype(jnp.float32) * (math.pi / (extent + 1))
    return jnp.sin(angles) * math.sqrt(2.0 / (extent + 1))


def axial_eigen(extent):
    indices = jnp.arange(extent, dtype=jnp.int32) + 1
    return 2.0 - 2.0 * jnp.cos(indices.astype(jnp.float32) * (math.pi / (extent + 1)))


def radial_basis(extent):
    mode_ids = jnp.arange(extent, dtype=jnp.int32)[:, None]
    cell_ids = jnp.arange(extent, dtype=jnp.int32)[None, :]
    phases = mode_ids * (2 * cell_ids + 1) % (4 * extent)
    angles = phases.astype(jnp.float32) * (math.pi / (2 * extent))
    weights = jnp.where(mode_ids == 0, math.sqrt(1.0 / extent), math.sqrt(2.0 / extent)).astype(
        jnp.float32
    )
    return jnp.cos(angles) * weights


def radial_eigen(mode_ids):
    return 2.0 - 2.0 * jnp.cos(mode_ids.astype(jnp.float32) * (math.pi / NR))


def cell_radius(cell_ids):
    return cell_ids.astype(jnp.float32) + (0.25 * NR + 0.5)


def fixed_azimuth_basis():
    positions = np.arange(NT)[:, None]
    modes = np.arange(NT)[None, :]
    frequency = np.where(modes <= NT // 2, modes, modes - NT // 2)
    angles = (positions * frequency % NT) * (2.0 * math.pi / NT)
    weights = np.where((modes == 0) | (modes == NT // 2), math.sqrt(1.0 / NT), math.sqrt(2.0 / NT))
    return (np.where(modes > NT // 2, np.sin(angles), np.cos(angles)) * weights).astype(np.float32)


def fixed_axial_basis():
    indices = np.arange(1, NX + 1)
    phases = indices[:, None] * indices[None, :] % (2 * (NX + 1))
    return (np.sin(phases * (math.pi / (NX + 1))) * math.sqrt(2.0 / (NX + 1))).astype(np.float32)


def fixed_radial_basis():
    modes = np.arange(NR)[:, None]
    cells = np.arange(NR)[None, :]
    angles = (modes * (2 * cells + 1) % (4 * NR)) * (math.pi / (2 * NR))
    weights = np.where(modes == 0, math.sqrt(1.0 / NR), math.sqrt(2.0 / NR))
    return (np.cos(angles) * weights).astype(np.float32)


AZIMUTH_TABLE = fixed_azimuth_basis()
AXIAL_TABLE = fixed_axial_basis()
RADIAL_TABLE = fixed_radial_basis()


def denominator_of(mode_ids, radial_ids):
    total = azimuth_eigen(mode_ids)[:, None, None] + axial_eigen(NX)[None, :, None]
    return total + radial_eigen(radial_ids)[None, None, :] + helmholtz_shift


def canopy_source(gore_map, rate_table):
    gore_ids = jnp.arange(rate_table.shape[0], dtype=jnp.int32)
    column_gore = jnp.arange(NT, dtype=jnp.int32) * GORES // NT
    matches = column_gore[:, None] == gore_ids[None, :]
    column_rate = jnp.sum(jnp.where(matches, rate_table[None, :], 0.0), axis=1)
    return jnp.where(gore_map < GORES, column_rate[None, None, :], 0.0)


def body(axial_vel, radial_vel, swirl_vel, inflow_rate, canopy_gore):
    radial_block = axial_vel.shape[1]
    axial_block = axial_vel.shape[0]
    row_index = lax.axis_index("row")
    row_count = lax.axis_size("row")
    gz_count = lax.axis_size("gz")
    both = ("gz", "row")
    device_count = gz_count * row_count
    spacing = 2.0 * math.pi / NT
    own_first = row_index * radial_block
    own_cells = own_first + jnp.arange(radial_block, dtype=jnp.int32)
    radius = cell_radius(own_cells)[None, :, None]
    axial_pad = jnp.pad(axial_vel, ((1, 1), (0, 0), (0, 0)))
    flux = radial_vel * radius
    if row_count == 2:
        edge_radius = jnp.where(row_index == 0, radius[:, -1:], radius[:, :1])
        edge_vel = jnp.where(row_index == 0, radial_vel[:, -1:], radial_vel[:, :1])
        received = lax.ppermute(edge_vel * edge_radius, "row", [(0, 1), (1, 0)])
        no_flux = jnp.zeros_like(received)
        low = jnp.where(row_index == 0, no_flux, received)
        high = jnp.where(row_index == 0, received, no_flux)
        radial_flux = jnp.concatenate([low, flux, high], axis=1)
    else:
        radial_flux = extended(flux, (("row", 1),), 1)
    divergence = 0.5 * (axial_pad[2:] - axial_pad[:-2])
    divergence = divergence + (radial_flux[:, 2:] - radial_flux[:, :-2]) / (2.0 * radius)
    divergence = divergence + (jnp.roll(swirl_vel, -1, 2) - jnp.roll(swirl_vel, 1, 2)) / (
        2.0 * radius * spacing
    )
    right_side = divergence - canopy_source(canopy_gore, inflow_rate)
    all_modes = jnp.arange(NT, dtype=jnp.int32)
    fourier = jnp.asarray(AZIMUTH_TABLE)
    planes = jnp.concatenate([right_side, axial_vel[:1], axial_vel[-1:]], axis=0)
    spectrum_in = jnp.einsum("xrt,tm->mxr", planes, fourier, precision=forward_precision)
    modes_each = NT // device_count
    spectrum_in = spectrum_in.reshape(device_count, modes_each, axial_block + 2, radial_block)
    resident = lax.all_to_all(spectrum_in, both, split_axis=0, concat_axis=0, tiled=True)
    resident = resident.reshape(gz_count, row_count, modes_each, axial_block + 2, radial_block)
    first_hat = resident[:, :, :, axial_block]
    last_hat = resident[:, :, :, axial_block + 1]
    next_first = jnp.concatenate([first_hat[1:], jnp.zeros_like(first_hat[:1])], axis=0)
    prev_last = jnp.concatenate([jnp.zeros_like(last_hat[:1]), last_hat[:-1]], axis=0)
    resident = resident[:, :, :, :axial_block]
    resident = resident.at[:, :, :, axial_block - 1].add(0.5 * next_first)
    resident = resident.at[:, :, :, 0].add(-0.5 * prev_last)
    mode_ids = lax.axis_index(both) * modes_each + jnp.arange(modes_each, dtype=jnp.int32)
    axial_table = jnp.asarray(AXIAL_TABLE).reshape(NX, gz_count, axial_block)
    radial_table = jnp.asarray(RADIAL_TABLE)
    axial_coefficient = jnp.einsum(
        "kgx,grmxj->mkrj", axial_table, resident, precision=forward_precision
    ).reshape(modes_each, NX, NR)
    spectrum = jnp.einsum("sj,mkj->mks", radial_table, axial_coefficient, precision=forward_precision)
    scaled = spectrum / denominator_of(mode_ids, jnp.arange(NR, dtype=jnp.int32))
    radial_returned = jnp.einsum("sj,mks->mkj", radial_table, scaled, precision=maximal_precision)
    radial_returned = radial_returned.reshape(modes_each, NX, row_count, radial_block)
    physical_space = jnp.einsum(
        "kgx,mkrj->grmxj", axial_table, radial_returned, precision=maximal_precision
    )
    first_p = physical_space[:, :, :, :1]
    last_p = physical_space[:, :, :, -1:]
    ghost_low = jnp.concatenate([jnp.zeros_like(last_p[:1]), last_p[:-1]], axis=0)
    ghost_high = jnp.concatenate([first_p[1:], jnp.zeros_like(first_p[:1])], axis=0)
    windows = jnp.concatenate([physical_space, ghost_low, ghost_high], axis=3)
    windows = windows.reshape(device_count, modes_each, axial_block + 2, radial_block)
    returned = lax.all_to_all(windows, both, split_axis=0, concat_axis=0, tiled=True)
    returned = returned.reshape(NT, axial_block + 2, radial_block)
    extended_p = -jnp.einsum("qxr,tq->xrt", returned, fourier, precision=maximal_precision)
    pressure = extended_p[:axial_block]
    padded = jnp.concatenate(
        [extended_p[axial_block : axial_block + 1], pressure, extended_p[axial_block + 1 :]], axis=0
    )
    if row_count == 2:
        sideways = radial_neighbour(pressure, pressure[:, :1], pressure[:, -1:])
        above = sideways[:, 2:]
        below = sideways[:, :-2]
    else:
        wide = extended(pressure, (("row", 1),), 1)
        lower_ghost = jnp.where(row_index == 0, pressure[:, :1], wide[:, :1])
        upper_ghost = jnp.where(row_index == row_count - 1, pressure[:, -1:], wide[:, -1:])
        above = jnp.concatenate([pressure[:, 1:], upper_ghost], axis=1)
        below = jnp.concatenate([lower_ghost, pressure[:, :-1]], axis=1)
    axial_out = axial_vel - 0.5 * (padded[2:] - padded[:-2])
    radial_projected_velocity = radial_vel - 0.5 * (above - below)
    swirl_out = swirl_vel - (jnp.roll(pressure, -1, 2) - jnp.roll(pressure, 1, 2)) / (
        2.0 * radius * spacing
    )
    return (axial_out, radial_projected_velocity, swirl_out)


def solution(mesh):
    placed = (
        P("gz", "row", None),
        P("gz", "row", None),
        P("gz", "row", None),
        P(),
        P("gz", "row", None),
    )
    return jax.shard_map(
        body,
        mesh=mesh,
        in_specs=placed,
        out_specs=(P("gz", "row", None), P("gz", "row", None), P("gz", "row", None)),
        check_vma=False,
    )
```

```python
import math

import numpy as np

import jax
import jax.numpy as jnp
from jax import lax
from jax.sharding import PartitionSpec as P

NX = 1024
NR = 256
NT = 256
GORES = 48


helmholtz_shift = 0.001
maximal_precision = lax.Precision.HIGHEST
forward_precision = lax.Precision.HIGH


def extended(block, sides, width):
    for axis, dim in sides:
        count = lax.axis_size(axis)
        forward = [(i, i + 1) for i in range(count - 1)]
        backward = [(target, source) for source, target in forward]
        low = lax.ppermute(
            lax.slice_in_dim(block, block.shape[dim] - width, None, axis=dim), axis, forward
        )
        high = lax.ppermute(lax.slice_in_dim(block, 0, width, axis=dim), axis, backward)
        block = jnp.concatenate([low, block, high], axis=dim)
    return block


def radial_neighbour(block, ghost_low, ghost_high):
    row_index = lax.axis_index("row")
    send = jnp.where(row_index == 0, block[:, -1:], block[:, :1])
    received = lax.ppermute(send, "row", [(0, 1), (1, 0)])
    low = jnp.where(row_index == 0, ghost_low, received)
    high = jnp.where(row_index == 0, received, ghost_high)
    return jnp.concatenate([low, block, high], axis=1)


def azimuth_basis(extent, mode_ids):
    positions = jnp.arange(extent, dtype=jnp.int32)
    half_way = extent // 2
    frequency = jnp.where(mode_ids <= half_way, mode_ids, mode_ids - half_way)
    phases = positions[:, None] * frequency[None, :] % extent
    angles = phases.astype(jnp.float32) * (2.0 * math.pi / extent)
    weights = jnp.where(
        (mode_ids == 0) | (mode_ids == half_way), math.sqrt(1.0 / extent), math.sqrt(2.0 / extent)
    ).astype(jnp.float32)
    return (
        jnp.where((mode_ids > half_way)[None, :], jnp.sin(angles), jnp.cos(angles))
        * weights[None, :]
    )


def azimuth_eigen(mode_ids):
    half_way = NT // 2
    frequency = jnp.where(mode_ids <= half_way, mode_ids, mode_ids - half_way)
    angles = frequency.astype(jnp.float32) * (2.0 * math.pi / NT)
    arc_step = 0.75 * NR * 2.0 * math.pi / NT
    return (2.0 - 2.0 * jnp.cos(angles)) / (arc_step * arc_step)


def axial_basis(extent):
    indices = jnp.arange(extent, dtype=jnp.int32) + 1
    phases = indices[:, None] * indices[None, :] % (2 * (extent + 1))
    angles = phases.astype(jnp.float32) * (math.pi / (extent + 1))
    return jnp.sin(angles) * math.sqrt(2.0 / (extent + 1))


def axial_eigen(extent):
    indices = jnp.arange(extent, dtype=jnp.int32) + 1
    return 2.0 - 2.0 * jnp.cos(indices.astype(jnp.float32) * (math.pi / (extent + 1)))


def radial_basis(extent):
    mode_ids = jnp.arange(extent, dtype=jnp.int32)[:, None]
    cell_ids = jnp.arange(extent, dtype=jnp.int32)[None, :]
    phases = mode_ids * (2 * cell_ids + 1) % (4 * extent)
    angles = phases.astype(jnp.float32) * (math.pi / (2 * extent))
    weights = jnp.where(mode_ids == 0, math.sqrt(1.0 / extent), math.sqrt(2.0 / extent)).astype(
        jnp.float32
    )
    return jnp.cos(angles) * weights


def radial_eigen(mode_ids):
    return 2.0 - 2.0 * jnp.cos(mode_ids.astype(jnp.float32) * (math.pi / NR))


def cell_radius(cell_ids):
    return cell_ids.astype(jnp.float32) + (0.25 * NR + 0.5)


def fixed_azimuth_basis():
    positions = np.arange(NT)[:, None]
    modes = np.arange(NT)[None, :]
    frequency = np.where(modes <= NT // 2, modes, modes - NT // 2)
    angles = (positions * frequency % NT) * (2.0 * math.pi / NT)
    weights = np.where((modes == 0) | (modes == NT // 2), math.sqrt(1.0 / NT), math.sqrt(2.0 / NT))
    return (np.where(modes > NT // 2, np.sin(angles), np.cos(angles)) * weights).astype(np.float32)


def fixed_axial_basis():
    indices = np.arange(1, NX + 1)
    phases = indices[:, None] * indices[None, :] % (2 * (NX + 1))
    return (np.sin(phases * (math.pi / (NX + 1))) * math.sqrt(2.0 / (NX + 1))).astype(np.float32)


def fixed_radial_basis():
    modes = np.arange(NR)[:, None]
    cells = np.arange(NR)[None, :]
    angles = (modes * (2 * cells + 1) % (4 * NR)) * (math.pi / (2 * NR))
    weights = np.where(modes == 0, math.sqrt(1.0 / NR), math.sqrt(2.0 / NR))
    return (np.cos(angles) * weights).astype(np.float32)


AZIMUTH_TABLE = fixed_azimuth_basis()
AXIAL_TABLE = fixed_axial_basis()


def halo_axial_tables(blocks):
    width = NX // blocks
    table = AXIAL_TABLE.reshape(NX, blocks, width)
    zero = np.zeros((NX, 1), np.float32)
    below = np.concatenate([zero, AXIAL_TABLE[:, width - 1 : NX - 1 : width]], axis=1)
    above = np.concatenate([AXIAL_TABLE[:, width::width], zero], axis=1)
    forward = np.concatenate([table, 0.5 * below[:, :, None], -0.5 * above[:, :, None]], axis=2)
    inverse = np.concatenate([table, below[:, :, None], above[:, :, None]], axis=2)
    return forward.astype(np.float32), inverse.astype(np.float32)
RADIAL_TABLE = fixed_radial_basis()


def denominator_of(mode_ids, radial_ids):
    total = azimuth_eigen(mode_ids)[:, None, None] + axial_eigen(NX)[None, :, None]
    return total + radial_eigen(radial_ids)[None, None, :] + helmholtz_shift


def canopy_source(gore_map, rate_table):
    gore_ids = jnp.arange(rate_table.shape[0], dtype=jnp.int32)
    column_gore = jnp.arange(NT, dtype=jnp.int32) * GORES // NT
    matches = column_gore[:, None] == gore_ids[None, :]
    column_rate = jnp.sum(jnp.where(matches, rate_table[None, :], 0.0), axis=1)
    return jnp.where(gore_map < GORES, column_rate[None, None, :], 0.0)


def body(axial_vel, radial_vel, swirl_vel, inflow_rate, canopy_gore):
    radial_block = axial_vel.shape[1]
    axial_block = axial_vel.shape[0]
    row_index = lax.axis_index("row")
    row_count = lax.axis_size("row")
    gz_count = lax.axis_size("gz")
    both = ("gz", "row")
    device_count = gz_count * row_count
    spacing = 2.0 * math.pi / NT
    own_first = row_index * radial_block
    own_cells = own_first + jnp.arange(radial_block, dtype=jnp.int32)
    radius = cell_radius(own_cells)[None, :, None]
    axial_pad = jnp.pad(axial_vel, ((1, 1), (0, 0), (0, 0)))
    flux = radial_vel * radius
    if row_count == 2:
        no_flux = jnp.zeros_like(flux[:, :1])
        radial_flux = radial_neighbour(flux, no_flux, no_flux)
    else:
        radial_flux = extended(flux, (("row", 1),), 1)
    divergence = 0.5 * (axial_pad[2:] - axial_pad[:-2])
    divergence = divergence + (radial_flux[:, 2:] - radial_flux[:, :-2]) / (2.0 * radius)
    divergence = divergence + (jnp.roll(swirl_vel, -1, 2) - jnp.roll(swirl_vel, 1, 2)) / (
        2.0 * radius * spacing
    )
    right_side = divergence - canopy_source(canopy_gore, inflow_rate)
    all_modes = jnp.arange(NT, dtype=jnp.int32)
    fourier = jnp.asarray(AZIMUTH_TABLE)
    planes = jnp.concatenate([right_side, axial_vel[:1], axial_vel[-1:]], axis=0)
    spectrum_in = jnp.einsum("xrt,tm->mxr", planes, fourier, precision=forward_precision)
    modes_each = NT // device_count
    spectrum_in = spectrum_in.reshape(device_count, modes_each, axial_block + 2, radial_block)
    resident = lax.all_to_all(spectrum_in, both, split_axis=0, concat_axis=0, tiled=True)
    resident = resident.reshape(gz_count, row_count, modes_each, axial_block + 2, radial_block)
    mode_ids = lax.axis_index(both) * modes_each + jnp.arange(modes_each, dtype=jnp.int32)
    forward_table, inverse_table = halo_axial_tables(gz_count)
    radial_table = jnp.asarray(RADIAL_TABLE)
    axial_coefficient = jnp.einsum(
        "kgx,grmxj->mkrj", jnp.asarray(forward_table), resident, precision=forward_precision
    ).reshape(modes_each, NX, NR)
    spectrum = jnp.einsum("sj,mkj->mks", radial_table, axial_coefficient, precision=forward_precision)
    scaled = spectrum / denominator_of(mode_ids, jnp.arange(NR, dtype=jnp.int32))
    radial_returned = jnp.einsum("sj,mks->mkj", radial_table, scaled, precision=maximal_precision)
    radial_returned = radial_returned.reshape(modes_each, NX, row_count, radial_block)
    windows = jnp.einsum(
        "kgx,mkrj->grmxj", jnp.asarray(inverse_table), radial_returned, precision=maximal_precision
    )
    windows = windows.reshape(device_count, modes_each, axial_block + 2, radial_block)
    returned = lax.all_to_all(windows, both, split_axis=0, concat_axis=0, tiled=True)
    returned = returned.reshape(NT, axial_block + 2, radial_block)
    extended_p = -jnp.einsum("qxr,tq->xrt", returned, fourier, precision=maximal_precision)
    pressure = extended_p[:axial_block]
    padded = jnp.concatenate(
        [extended_p[axial_block : axial_block + 1], pressure, extended_p[axial_block + 1 :]], axis=0
    )
    if row_count == 2:
        sideways = radial_neighbour(pressure, pressure[:, :1], pressure[:, -1:])
        above = sideways[:, 2:]
        below = sideways[:, :-2]
    else:
        wide = extended(pressure, (("row", 1),), 1)
        lower_ghost = jnp.where(row_index == 0, pressure[:, :1], wide[:, :1])
        upper_ghost = jnp.where(row_index == row_count - 1, pressure[:, -1:], wide[:, -1:])
        above = jnp.concatenate([pressure[:, 1:], upper_ghost], axis=1)
        below = jnp.concatenate([lower_ghost, pressure[:, :-1]], axis=1)
    axial_out = axial_vel - 0.5 * (padded[2:] - padded[:-2])
    radial_projected_velocity = radial_vel - 0.5 * (above - below)
    swirl_out = swirl_vel - (jnp.roll(pressure, -1, 2) - jnp.roll(pressure, 1, 2)) / (
        2.0 * radius * spacing
    )
    return (axial_out, radial_projected_velocity, swirl_out)


def solution(mesh):
    placed = (
        P("gz", "row", None),
        P("gz", "row", None),
        P("gz", "row", None),
        P(),
        P("gz", "row", None),
    )
    return jax.shard_map(
        body,
        mesh=mesh,
        in_specs=placed,
        out_specs=(P("gz", "row", None), P("gz", "row", None), P("gz", "row", None)),
        check_vma=False,
    )
```

```python
import math

import numpy as np

import jax
import jax.numpy as jnp
from jax import lax
from jax.sharding import PartitionSpec as P

NX = 1024
NR = 256
NT = 256
GORES = 48


helmholtz_shift = 0.001
maximal_precision = lax.Precision.HIGHEST
forward_precision = lax.Precision.HIGH


def extended(block, sides, width):
    for axis, dim in sides:
        count = lax.axis_size(axis)
        forward = [(i, i + 1) for i in range(count - 1)]
        backward = [(target, source) for source, target in forward]
        low = lax.ppermute(
            lax.slice_in_dim(block, block.shape[dim] - width, None, axis=dim), axis, forward
        )
        high = lax.ppermute(lax.slice_in_dim(block, 0, width, axis=dim), axis, backward)
        block = jnp.concatenate([low, block, high], axis=dim)
    return block


def radial_neighbour(block, ghost_low, ghost_high):
    row_index = lax.axis_index("row")
    send = jnp.where(row_index == 0, block[:, -1:], block[:, :1])
    received = lax.ppermute(send, "row", [(0, 1), (1, 0)])
    low = jnp.where(row_index == 0, ghost_low, received)
    high = jnp.where(row_index == 0, received, ghost_high)
    return jnp.concatenate([low, block, high], axis=1)


def azimuth_basis(extent, mode_ids):
    positions = jnp.arange(extent, dtype=jnp.int32)
    half_way = extent // 2
    frequency = jnp.where(mode_ids <= half_way, mode_ids, mode_ids - half_way)
    phases = positions[:, None] * frequency[None, :] % extent
    angles = phases.astype(jnp.float32) * (2.0 * math.pi / extent)
    weights = jnp.where(
        (mode_ids == 0) | (mode_ids == half_way), math.sqrt(1.0 / extent), math.sqrt(2.0 / extent)
    ).astype(jnp.float32)
    return (
        jnp.where((mode_ids > half_way)[None, :], jnp.sin(angles), jnp.cos(angles))
        * weights[None, :]
    )


def azimuth_eigen(mode_ids):
    half_way = NT // 2
    frequency = jnp.where(mode_ids <= half_way, mode_ids, mode_ids - half_way)
    angles = frequency.astype(jnp.float32) * (2.0 * math.pi / NT)
    arc_step = 0.75 * NR * 2.0 * math.pi / NT
    return (2.0 - 2.0 * jnp.cos(angles)) / (arc_step * arc_step)


def axial_basis(extent):
    indices = jnp.arange(extent, dtype=jnp.int32) + 1
    phases = indices[:, None] * indices[None, :] % (2 * (extent + 1))
    angles = phases.astype(jnp.float32) * (math.pi / (extent + 1))
    return jnp.sin(angles) * math.sqrt(2.0 / (extent + 1))


def axial_eigen(extent):
    indices = jnp.arange(extent, dtype=jnp.int32) + 1
    return 2.0 - 2.0 * jnp.cos(indices.astype(jnp.float32) * (math.pi / (extent + 1)))


def radial_basis(extent):
    mode_ids = jnp.arange(extent, dtype=jnp.int32)[:, None]
    cell_ids = jnp.arange(extent, dtype=jnp.int32)[None, :]
    phases = mode_ids * (2 * cell_ids + 1) % (4 * extent)
    angles = phases.astype(jnp.float32) * (math.pi / (2 * extent))
    weights = jnp.where(mode_ids == 0, math.sqrt(1.0 / extent), math.sqrt(2.0 / extent)).astype(
        jnp.float32
    )
    return jnp.cos(angles) * weights


def radial_eigen(mode_ids):
    return 2.0 - 2.0 * jnp.cos(mode_ids.astype(jnp.float32) * (math.pi / NR))


def cell_radius(cell_ids):
    return cell_ids.astype(jnp.float32) + (0.25 * NR + 0.5)


def fixed_azimuth_basis():
    positions = np.arange(NT)[:, None]
    modes = np.arange(NT)[None, :]
    frequency = np.where(modes <= NT // 2, modes, modes - NT // 2)
    angles = (positions * frequency % NT) * (2.0 * math.pi / NT)
    weights = np.where((modes == 0) | (modes == NT // 2), math.sqrt(1.0 / NT), math.sqrt(2.0 / NT))
    return (np.where(modes > NT // 2, np.sin(angles), np.cos(angles)) * weights).astype(np.float32)


def fixed_axial_basis():
    indices = np.arange(1, NX + 1)
    phases = indices[:, None] * indices[None, :] % (2 * (NX + 1))
    return (np.sin(phases * (math.pi / (NX + 1))) * math.sqrt(2.0 / (NX + 1))).astype(np.float32)


def fixed_radial_basis():
    modes = np.arange(NR)[:, None]
    cells = np.arange(NR)[None, :]
    angles = (modes * (2 * cells + 1) % (4 * NR)) * (math.pi / (2 * NR))
    weights = np.where(modes == 0, math.sqrt(1.0 / NR), math.sqrt(2.0 / NR))
    return (np.cos(angles) * weights).astype(np.float32)


AZIMUTH_TABLE = fixed_azimuth_basis()
AXIAL_TABLE = fixed_axial_basis()


def halo_axial_tables(blocks):
    width = NX // blocks
    table = AXIAL_TABLE.reshape(NX, blocks, width)
    zero = np.zeros((NX, 1), np.float32)
    below = np.concatenate([zero, AXIAL_TABLE[:, width - 1 : NX - 1 : width]], axis=1)
    above = np.concatenate([AXIAL_TABLE[:, width::width], zero], axis=1)
    forward = np.concatenate([table, 0.5 * below[:, :, None], -0.5 * above[:, :, None]], axis=2)
    inverse = np.concatenate([table, below[:, :, None], above[:, :, None]], axis=2)
    return forward.astype(np.float32), inverse.astype(np.float32)
RADIAL_TABLE = fixed_radial_basis()


def denominator_of(mode_ids, radial_ids):
    total = azimuth_eigen(mode_ids)[:, None, None] + axial_eigen(NX)[None, :, None]
    return total + radial_eigen(radial_ids)[None, None, :] + helmholtz_shift


def canopy_source(gore_map, rate_table):
    gore_ids = jnp.arange(rate_table.shape[0], dtype=jnp.int32)
    column_gore = jnp.arange(NT, dtype=jnp.int32) * GORES // NT
    matches = column_gore[:, None] == gore_ids[None, :]
    column_rate = jnp.sum(jnp.where(matches, rate_table[None, :], 0.0), axis=1)
    return jnp.where(gore_map < GORES, column_rate[None, None, :], 0.0)


def body(axial_vel, radial_vel, swirl_vel, inflow_rate, canopy_gore):
    radial_block = axial_vel.shape[1]
    axial_block = axial_vel.shape[0]
    row_index = lax.axis_index("row")
    row_count = lax.axis_size("row")
    gz_count = lax.axis_size("gz")
    both = ("gz", "row")
    device_count = gz_count * row_count
    spacing = 2.0 * math.pi / NT
    own_first = row_index * radial_block
    own_cells = own_first + jnp.arange(radial_block, dtype=jnp.int32)
    radius = cell_radius(own_cells)[None, :, None]
    axial_pad = jnp.pad(axial_vel, ((1, 1), (0, 0), (0, 0)))
    flux = radial_vel * radius
    if row_count == 2:
        no_flux = jnp.zeros_like(flux[:, :1])
        radial_flux = radial_neighbour(flux, no_flux, no_flux)
    else:
        radial_flux = extended(flux, (("row", 1),), 1)
    divergence = 0.5 * (axial_pad[2:] - axial_pad[:-2])
    divergence = divergence + (radial_flux[:, 2:] - radial_flux[:, :-2]) / (2.0 * radius)
    divergence = divergence + (jnp.roll(swirl_vel, -1, 2) - jnp.roll(swirl_vel, 1, 2)) / (
        2.0 * radius * spacing
    )
    right_side = divergence - canopy_source(canopy_gore, inflow_rate)
    all_modes = jnp.arange(NT, dtype=jnp.int32)
    fourier = jnp.asarray(AZIMUTH_TABLE)
    planes = jnp.concatenate([right_side, axial_vel[:1], axial_vel[-1:]], axis=0)
    spectrum_in = jnp.einsum("xrt,tm->mxr", planes, fourier, precision=forward_precision)
    modes_each = NT // device_count
    spectrum_in = spectrum_in.reshape(device_count, modes_each, axial_block + 2, radial_block)
    resident = lax.all_to_all(spectrum_in, both, split_axis=0, concat_axis=0, tiled=True)
    resident = resident.reshape(gz_count, row_count, modes_each, axial_block + 2, radial_block)
    mode_ids = lax.axis_index(both) * modes_each + jnp.arange(modes_each, dtype=jnp.int32)
    forward_table = halo_axial_tables(gz_count)[0]
    radial_table = jnp.asarray(RADIAL_TABLE)
    axial_coefficient = jnp.einsum(
        "kgx,grmxj->mkrj", jnp.asarray(forward_table), resident, precision=forward_precision
    ).reshape(modes_each, NX, NR)
    spectrum = jnp.einsum("sj,mkj->mks", radial_table, axial_coefficient, precision=forward_precision)
    scaled = spectrum / denominator_of(mode_ids, jnp.arange(NR, dtype=jnp.int32))
    radial_returned = jnp.einsum("sj,mks->mkj", radial_table, scaled, precision=maximal_precision)
    radial_returned = radial_returned.reshape(modes_each, NX, row_count, radial_block)
    physical_space = jnp.einsum(
        "kgx,mkrj->grmxj",
        jnp.asarray(AXIAL_TABLE).reshape(NX, gz_count, axial_block),
        radial_returned,
        precision=maximal_precision,
    )
    first_p = physical_space[:, :, :, :1]
    last_p = physical_space[:, :, :, -1:]
    ghost_low = jnp.concatenate([jnp.zeros_like(last_p[:1]), last_p[:-1]], axis=0)
    ghost_high = jnp.concatenate([first_p[1:], jnp.zeros_like(first_p[:1])], axis=0)
    windows = jnp.concatenate([physical_space, ghost_low, ghost_high], axis=3)
    windows = windows.reshape(device_count, modes_each, axial_block + 2, radial_block)
    returned = lax.all_to_all(windows, both, split_axis=0, concat_axis=0, tiled=True)
    returned = returned.reshape(NT, axial_block + 2, radial_block)
    extended_p = -jnp.einsum("qxr,tq->xrt", returned, fourier, precision=maximal_precision)
    pressure = extended_p[:axial_block]
    padded = jnp.concatenate(
        [extended_p[axial_block : axial_block + 1], pressure, extended_p[axial_block + 1 :]], axis=0
    )
    if row_count == 2:
        sideways = radial_neighbour(pressure, pressure[:, :1], pressure[:, -1:])
        above = sideways[:, 2:]
        below = sideways[:, :-2]
    else:
        wide = extended(pressure, (("row", 1),), 1)
        lower_ghost = jnp.where(row_index == 0, pressure[:, :1], wide[:, :1])
        upper_ghost = jnp.where(row_index == row_count - 1, pressure[:, -1:], wide[:, -1:])
        above = jnp.concatenate([pressure[:, 1:], upper_ghost], axis=1)
        below = jnp.concatenate([lower_ghost, pressure[:, :-1]], axis=1)
    axial_out = axial_vel - 0.5 * (padded[2:] - padded[:-2])
    radial_projected_velocity = radial_vel - 0.5 * (above - below)
    swirl_out = swirl_vel - (jnp.roll(pressure, -1, 2) - jnp.roll(pressure, 1, 2)) / (
        2.0 * radius * spacing
    )
    return (axial_out, radial_projected_velocity, swirl_out)


def solution(mesh):
    placed = (
        P("gz", "row", None),
        P("gz", "row", None),
        P("gz", "row", None),
        P(),
        P("gz", "row", None),
    )
    return jax.shard_map(
        body,
        mesh=mesh,
        in_specs=placed,
        out_specs=(P("gz", "row", None), P("gz", "row", None), P("gz", "row", None)),
        check_vma=False,
    )
```

```python
import math

import numpy as np

import jax
import jax.numpy as jnp
from jax import lax
from jax.sharding import PartitionSpec as P

NX = 1024
NR = 256
NT = 256
GORES = 48


helmholtz_shift = 0.001
maximal_precision = lax.Precision.HIGHEST
forward_precision = lax.Precision.HIGH


def extended(block, sides, width):
    for axis, dim in sides:
        count = lax.axis_size(axis)
        forward = [(i, i + 1) for i in range(count - 1)]
        backward = [(target, source) for source, target in forward]
        low = lax.ppermute(
            lax.slice_in_dim(block, block.shape[dim] - width, None, axis=dim), axis, forward
        )
        high = lax.ppermute(lax.slice_in_dim(block, 0, width, axis=dim), axis, backward)
        block = jnp.concatenate([low, block, high], axis=dim)
    return block


def radial_neighbour(block, ghost_low, ghost_high):
    row_index = lax.axis_index("row")
    send = jnp.where(row_index == 0, block[:, -1:], block[:, :1])
    received = lax.ppermute(send, "row", [(0, 1), (1, 0)])
    low = jnp.where(row_index == 0, ghost_low, received)
    high = jnp.where(row_index == 0, received, ghost_high)
    return jnp.concatenate([low, block, high], axis=1)


def azimuth_basis(extent, mode_ids):
    positions = jnp.arange(extent, dtype=jnp.int32)
    half_way = extent // 2
    frequency = jnp.where(mode_ids <= half_way, mode_ids, mode_ids - half_way)
    phases = positions[:, None] * frequency[None, :] % extent
    angles = phases.astype(jnp.float32) * (2.0 * math.pi / extent)
    weights = jnp.where(
        (mode_ids == 0) | (mode_ids == half_way), math.sqrt(1.0 / extent), math.sqrt(2.0 / extent)
    ).astype(jnp.float32)
    return (
        jnp.where((mode_ids > half_way)[None, :], jnp.sin(angles), jnp.cos(angles))
        * weights[None, :]
    )


def azimuth_eigen(mode_ids):
    half_way = NT // 2
    frequency = jnp.where(mode_ids <= half_way, mode_ids, mode_ids - half_way)
    angles = frequency.astype(jnp.float32) * (2.0 * math.pi / NT)
    arc_step = 0.75 * NR * 2.0 * math.pi / NT
    return (2.0 - 2.0 * jnp.cos(angles)) / (arc_step * arc_step)


def axial_basis(extent):
    indices = jnp.arange(extent, dtype=jnp.int32) + 1
    phases = indices[:, None] * indices[None, :] % (2 * (extent + 1))
    angles = phases.astype(jnp.float32) * (math.pi / (extent + 1))
    return jnp.sin(angles) * math.sqrt(2.0 / (extent + 1))


def axial_eigen(extent):
    indices = jnp.arange(extent, dtype=jnp.int32) + 1
    return 2.0 - 2.0 * jnp.cos(indices.astype(jnp.float32) * (math.pi / (extent + 1)))


def radial_basis(extent):
    mode_ids = jnp.arange(extent, dtype=jnp.int32)[:, None]
    cell_ids = jnp.arange(extent, dtype=jnp.int32)[None, :]
    phases = mode_ids * (2 * cell_ids + 1) % (4 * extent)
    angles = phases.astype(jnp.float32) * (math.pi / (2 * extent))
    weights = jnp.where(mode_ids == 0, math.sqrt(1.0 / extent), math.sqrt(2.0 / extent)).astype(
        jnp.float32
    )
    return jnp.cos(angles) * weights


def radial_eigen(mode_ids):
    return 2.0 - 2.0 * jnp.cos(mode_ids.astype(jnp.float32) * (math.pi / NR))


def cell_radius(cell_ids):
    return cell_ids.astype(jnp.float32) + (0.25 * NR + 0.5)


def fixed_azimuth_basis():
    positions = np.arange(NT)[:, None]
    modes = np.arange(NT)[None, :]
    frequency = np.where(modes <= NT // 2, modes, modes - NT // 2)
    angles = (positions * frequency % NT) * (2.0 * math.pi / NT)
    weights = np.where((modes == 0) | (modes == NT // 2), math.sqrt(1.0 / NT), math.sqrt(2.0 / NT))
    return (np.where(modes > NT // 2, np.sin(angles), np.cos(angles)) * weights).astype(np.float32)


def fixed_axial_basis():
    indices = np.arange(1, NX + 1)
    phases = indices[:, None] * indices[None, :] % (2 * (NX + 1))
    return (np.sin(phases * (math.pi / (NX + 1))) * math.sqrt(2.0 / (NX + 1))).astype(np.float32)


def fixed_radial_basis():
    modes = np.arange(NR)[:, None]
    cells = np.arange(NR)[None, :]
    angles = (modes * (2 * cells + 1) % (4 * NR)) * (math.pi / (2 * NR))
    weights = np.where(modes == 0, math.sqrt(1.0 / NR), math.sqrt(2.0 / NR))
    return (np.cos(angles) * weights).astype(np.float32)


AZIMUTH_TABLE = fixed_azimuth_basis()
AXIAL_TABLE = fixed_axial_basis()


def halo_axial_tables(blocks):
    width = NX // blocks
    table = AXIAL_TABLE.reshape(NX, blocks, width)
    zero = np.zeros((NX, 1), np.float32)
    below = np.concatenate([zero, AXIAL_TABLE[:, width - 1 : NX - 1 : width]], axis=1)
    above = np.concatenate([AXIAL_TABLE[:, width::width], zero], axis=1)
    forward = np.concatenate([table, 0.5 * below[:, :, None], -0.5 * above[:, :, None]], axis=2)
    inverse = np.concatenate([table, below[:, :, None], above[:, :, None]], axis=2)
    return forward.astype(np.float32), inverse.astype(np.float32)
RADIAL_TABLE = fixed_radial_basis()


def denominator_of(mode_ids, radial_ids):
    total = azimuth_eigen(mode_ids)[:, None, None] + axial_eigen(NX)[None, :, None]
    return total + radial_eigen(radial_ids)[None, None, :] + helmholtz_shift


def canopy_source(gore_map, rate_table):
    gore_ids = jnp.arange(rate_table.shape[0], dtype=jnp.int32)
    column_gore = jnp.arange(NT, dtype=jnp.int32) * GORES // NT
    matches = column_gore[:, None] == gore_ids[None, :]
    column_rate = jnp.sum(jnp.where(matches, rate_table[None, :], 0.0), axis=1)
    return jnp.where(gore_map < GORES, column_rate[None, None, :], 0.0)


def body(axial_vel, radial_vel, swirl_vel, inflow_rate, canopy_gore):
    radial_block = axial_vel.shape[1]
    axial_block = axial_vel.shape[0]
    row_index = lax.axis_index("row")
    row_count = lax.axis_size("row")
    gz_count = lax.axis_size("gz")
    both = ("gz", "row")
    device_count = gz_count * row_count
    spacing = 2.0 * math.pi / NT
    own_first = row_index * radial_block
    own_cells = own_first + jnp.arange(radial_block, dtype=jnp.int32)
    radius = cell_radius(own_cells)[None, :, None]
    axial_pad = jnp.pad(axial_vel, ((1, 1), (0, 0), (0, 0)))
    if row_count == 2:
        send = jnp.where(row_index == 0, radial_vel[:, -1:], radial_vel[:, :1])
        received = lax.ppermute(send, "row", [(0, 1), (1, 0)])
        no_vel = jnp.zeros_like(received)
        low = jnp.where(row_index == 0, no_vel, received)
        high = jnp.where(row_index == 0, received, no_vel)
        up = jnp.concatenate([radial_vel[:, 1:], high], axis=1) * cell_radius(own_cells + 1)[None, :, None]
        down = jnp.concatenate([low, radial_vel[:, :-1]], axis=1) * cell_radius(own_cells - 1)[None, :, None]
        radial_term = (up - down) / (2.0 * radius)
    else:
        flux = radial_vel * radius
        radial_flux = extended(flux, (("row", 1),), 1)
        radial_term = (radial_flux[:, 2:] - radial_flux[:, :-2]) / (2.0 * radius)
    divergence = 0.5 * (axial_pad[2:] - axial_pad[:-2])
    divergence = divergence + radial_term
    divergence = divergence + (jnp.roll(swirl_vel, -1, 2) - jnp.roll(swirl_vel, 1, 2)) / (
        2.0 * radius * spacing
    )
    right_side = divergence - canopy_source(canopy_gore, inflow_rate)
    all_modes = jnp.arange(NT, dtype=jnp.int32)
    fourier = jnp.asarray(AZIMUTH_TABLE)
    planes = jnp.concatenate([right_side, axial_vel[:1], axial_vel[-1:]], axis=0)
    spectrum_in = jnp.einsum("xrt,tm->mxr", planes, fourier, precision=forward_precision)
    modes_each = NT // device_count
    spectrum_in = spectrum_in.reshape(device_count, modes_each, axial_block + 2, radial_block)
    resident = lax.all_to_all(spectrum_in, both, split_axis=0, concat_axis=0, tiled=True)
    resident = resident.reshape(gz_count, row_count, modes_each, axial_block + 2, radial_block)
    mode_ids = lax.axis_index(both) * modes_each + jnp.arange(modes_each, dtype=jnp.int32)
    forward_table = halo_axial_tables(gz_count)[0]
    radial_table = jnp.asarray(RADIAL_TABLE)
    axial_coefficient = jnp.einsum(
        "kgx,grmxj->mkrj", jnp.asarray(forward_table), resident, precision=forward_precision
    ).reshape(modes_each, NX, NR)
    spectrum = jnp.einsum("sj,mkj->mks", radial_table, axial_coefficient, precision=forward_precision)
    scaled = spectrum / denominator_of(mode_ids, jnp.arange(NR, dtype=jnp.int32))
    radial_returned = jnp.einsum("sj,mks->mkj", radial_table, scaled, precision=maximal_precision)
    radial_returned = radial_returned.reshape(modes_each, NX, row_count, radial_block)
    physical_space = jnp.einsum(
        "kgx,mkrj->grmxj",
        jnp.asarray(AXIAL_TABLE).reshape(NX, gz_count, axial_block),
        radial_returned,
        precision=maximal_precision,
    )
    first_p = physical_space[:, :, :, :1]
    last_p = physical_space[:, :, :, -1:]
    ghost_low = jnp.concatenate([jnp.zeros_like(last_p[:1]), last_p[:-1]], axis=0)
    ghost_high = jnp.concatenate([first_p[1:], jnp.zeros_like(first_p[:1])], axis=0)
    windows = jnp.concatenate([physical_space, ghost_low, ghost_high], axis=3)
    windows = windows.reshape(device_count, modes_each, axial_block + 2, radial_block)
    returned = lax.all_to_all(windows, both, split_axis=0, concat_axis=0, tiled=True)
    returned = returned.reshape(NT, axial_block + 2, radial_block)
    extended_p = -jnp.einsum("qxr,tq->xrt", returned, fourier, precision=maximal_precision)
    pressure = extended_p[:axial_block]
    padded = jnp.concatenate(
        [extended_p[axial_block : axial_block + 1], pressure, extended_p[axial_block + 1 :]], axis=0
    )
    if row_count == 2:
        sideways = radial_neighbour(pressure, pressure[:, :1], pressure[:, -1:])
        above = sideways[:, 2:]
        below = sideways[:, :-2]
    else:
        wide = extended(pressure, (("row", 1),), 1)
        lower_ghost = jnp.where(row_index == 0, pressure[:, :1], wide[:, :1])
        upper_ghost = jnp.where(row_index == row_count - 1, pressure[:, -1:], wide[:, -1:])
        above = jnp.concatenate([pressure[:, 1:], upper_ghost], axis=1)
        below = jnp.concatenate([lower_ghost, pressure[:, :-1]], axis=1)
    axial_out = axial_vel - 0.5 * (padded[2:] - padded[:-2])
    radial_projected_velocity = radial_vel - 0.5 * (above - below)
    swirl_out = swirl_vel - (jnp.roll(pressure, -1, 2) - jnp.roll(pressure, 1, 2)) / (
        2.0 * radius * spacing
    )
    return (axial_out, radial_projected_velocity, swirl_out)


def solution(mesh):
    placed = (
        P("gz", "row", None),
        P("gz", "row", None),
        P("gz", "row", None),
        P(),
        P("gz", "row", None),
    )
    return jax.shard_map(
        body,
        mesh=mesh,
        in_specs=placed,
        out_specs=(P("gz", "row", None), P("gz", "row", None), P("gz", "row", None)),
        check_vma=False,
    )
```

```python
import math

import numpy as np

import jax
import jax.numpy as jnp
from jax import lax
from jax.sharding import PartitionSpec as P

NX = 1024
NR = 256
NT = 256
GORES = 48


helmholtz_shift = 0.001
maximal_precision = lax.Precision.HIGHEST
forward_precision = lax.Precision.HIGH


def extended(block, sides, width):
    for axis, dim in sides:
        count = lax.axis_size(axis)
        forward = [(i, i + 1) for i in range(count - 1)]
        backward = [(target, source) for source, target in forward]
        low = lax.ppermute(
            lax.slice_in_dim(block, block.shape[dim] - width, None, axis=dim), axis, forward
        )
        high = lax.ppermute(lax.slice_in_dim(block, 0, width, axis=dim), axis, backward)
        block = jnp.concatenate([low, block, high], axis=dim)
    return block


def radial_neighbour(block, ghost_low, ghost_high):
    row_index = lax.axis_index("row")
    send = jnp.where(row_index == 0, block[:, -1:], block[:, :1])
    received = lax.ppermute(send, "row", [(0, 1), (1, 0)])
    low = jnp.where(row_index == 0, ghost_low, received)
    high = jnp.where(row_index == 0, received, ghost_high)
    return jnp.concatenate([low, block, high], axis=1)


def azimuth_basis(extent, mode_ids):
    positions = jnp.arange(extent, dtype=jnp.int32)
    half_way = extent // 2
    frequency = jnp.where(mode_ids <= half_way, mode_ids, mode_ids - half_way)
    phases = positions[:, None] * frequency[None, :] % extent
    angles = phases.astype(jnp.float32) * (2.0 * math.pi / extent)
    weights = jnp.where(
        (mode_ids == 0) | (mode_ids == half_way), math.sqrt(1.0 / extent), math.sqrt(2.0 / extent)
    ).astype(jnp.float32)
    return (
        jnp.where((mode_ids > half_way)[None, :], jnp.sin(angles), jnp.cos(angles))
        * weights[None, :]
    )


def azimuth_eigen(mode_ids):
    half_way = NT // 2
    frequency = jnp.where(mode_ids <= half_way, mode_ids, mode_ids - half_way)
    angles = frequency.astype(jnp.float32) * (2.0 * math.pi / NT)
    arc_step = 0.75 * NR * 2.0 * math.pi / NT
    return (2.0 - 2.0 * jnp.cos(angles)) / (arc_step * arc_step)


def axial_basis(extent):
    indices = jnp.arange(extent, dtype=jnp.int32) + 1
    phases = indices[:, None] * indices[None, :] % (2 * (extent + 1))
    angles = phases.astype(jnp.float32) * (math.pi / (extent + 1))
    return jnp.sin(angles) * math.sqrt(2.0 / (extent + 1))


def axial_eigen(extent):
    indices = jnp.arange(extent, dtype=jnp.int32) + 1
    return 2.0 - 2.0 * jnp.cos(indices.astype(jnp.float32) * (math.pi / (extent + 1)))


def radial_basis(extent):
    mode_ids = jnp.arange(extent, dtype=jnp.int32)[:, None]
    cell_ids = jnp.arange(extent, dtype=jnp.int32)[None, :]
    phases = mode_ids * (2 * cell_ids + 1) % (4 * extent)
    angles = phases.astype(jnp.float32) * (math.pi / (2 * extent))
    weights = jnp.where(mode_ids == 0, math.sqrt(1.0 / extent), math.sqrt(2.0 / extent)).astype(
        jnp.float32
    )
    return jnp.cos(angles) * weights


def radial_eigen(mode_ids):
    return 2.0 - 2.0 * jnp.cos(mode_ids.astype(jnp.float32) * (math.pi / NR))


def cell_radius(cell_ids):
    return cell_ids.astype(jnp.float32) + (0.25 * NR + 0.5)


def fixed_azimuth_basis():
    positions = np.arange(NT)[:, None]
    modes = np.arange(NT)[None, :]
    frequency = np.where(modes <= NT // 2, modes, modes - NT // 2)
    angles = (positions * frequency % NT) * (2.0 * math.pi / NT)
    weights = np.where((modes == 0) | (modes == NT // 2), math.sqrt(1.0 / NT), math.sqrt(2.0 / NT))
    return (np.where(modes > NT // 2, np.sin(angles), np.cos(angles)) * weights).astype(np.float32)


def fixed_axial_basis():
    indices = np.arange(1, NX + 1)
    phases = indices[:, None] * indices[None, :] % (2 * (NX + 1))
    return (np.sin(phases * (math.pi / (NX + 1))) * math.sqrt(2.0 / (NX + 1))).astype(np.float32)


def fixed_radial_basis():
    modes = np.arange(NR)[:, None]
    cells = np.arange(NR)[None, :]
    angles = (modes * (2 * cells + 1) % (4 * NR)) * (math.pi / (2 * NR))
    weights = np.where(modes == 0, math.sqrt(1.0 / NR), math.sqrt(2.0 / NR))
    return (np.cos(angles) * weights).astype(np.float32)


AZIMUTH_TABLE = fixed_azimuth_basis()
AXIAL_TABLE = fixed_axial_basis()


def halo_axial_tables(blocks):
    width = NX // blocks
    table = AXIAL_TABLE.reshape(NX, blocks, width)
    zero = np.zeros((NX, 1), np.float32)
    below = np.concatenate([zero, AXIAL_TABLE[:, width - 1 : NX - 1 : width]], axis=1)
    above = np.concatenate([AXIAL_TABLE[:, width::width], zero], axis=1)
    forward = np.concatenate([table, 0.5 * below[:, :, None], -0.5 * above[:, :, None]], axis=2)
    inverse = np.concatenate([table, below[:, :, None], above[:, :, None]], axis=2)
    return forward.astype(np.float32), inverse.astype(np.float32)
RADIAL_TABLE = fixed_radial_basis()


def denominator_of(mode_ids, radial_ids):
    total = azimuth_eigen(mode_ids)[:, None, None] + axial_eigen(NX)[None, :, None]
    return total + radial_eigen(radial_ids)[None, None, :] + helmholtz_shift


def canopy_source(gore_map, rate_table):
    gore_ids = jnp.arange(rate_table.shape[0], dtype=jnp.int32)
    column_gore = jnp.arange(NT, dtype=jnp.int32) * GORES // NT
    matches = column_gore[:, None] == gore_ids[None, :]
    column_rate = jnp.sum(jnp.where(matches, rate_table[None, :], 0.0), axis=1)
    return jnp.where(gore_map < GORES, column_rate[None, None, :], 0.0)


def body(axial_vel, radial_vel, swirl_vel, inflow_rate, canopy_gore):
    radial_block = axial_vel.shape[1]
    axial_block = axial_vel.shape[0]
    row_index = lax.axis_index("row")
    row_count = lax.axis_size("row")
    gz_count = lax.axis_size("gz")
    both = ("gz", "row")
    device_count = gz_count * row_count
    spacing = 2.0 * math.pi / NT
    own_first = row_index * radial_block
    own_cells = own_first + jnp.arange(radial_block, dtype=jnp.int32)
    radius = cell_radius(own_cells)[None, :, None]
    axial_pad = jnp.pad(axial_vel, ((1, 1), (0, 0), (0, 0)))
    flux = radial_vel * radius
    if row_count == 2:
        no_flux = jnp.zeros_like(flux[:, :1])
        radial_flux = radial_neighbour(flux, no_flux, no_flux)
    else:
        radial_flux = extended(flux, (("row", 1),), 1)
    divergence = 0.5 * (axial_pad[2:] - axial_pad[:-2])
    divergence = divergence + (radial_flux[:, 2:] - radial_flux[:, :-2]) / (2.0 * radius)
    divergence = divergence + (jnp.roll(swirl_vel, -1, 2) - jnp.roll(swirl_vel, 1, 2)) / (
        2.0 * radius * spacing
    )
    right_side = divergence - canopy_source(canopy_gore, inflow_rate)
    all_modes = jnp.arange(NT, dtype=jnp.int32)
    fourier = jnp.asarray(AZIMUTH_TABLE)
    planes = jnp.concatenate([right_side, axial_vel[:1], axial_vel[-1:]], axis=0)
    spectrum_in = jnp.einsum("xrt,tm->mxr", planes, fourier, precision=forward_precision)
    modes_each = NT // device_count
    spectrum_in = spectrum_in.reshape(device_count, modes_each, axial_block + 2, radial_block)
    resident = lax.all_to_all(spectrum_in, both, split_axis=0, concat_axis=0, tiled=True)
    resident = resident.reshape(gz_count, row_count, modes_each, axial_block + 2, radial_block)
    mode_ids = lax.axis_index(both) * modes_each + jnp.arange(modes_each, dtype=jnp.int32)
    forward_table = halo_axial_tables(gz_count)[0]
    radial_table = jnp.asarray(RADIAL_TABLE)
    axial_coefficient = jnp.einsum(
        "kgx,grmxj->mkrj", jnp.asarray(forward_table), resident, precision=forward_precision
    ).reshape(modes_each, NX, NR)
    spectrum = jnp.einsum("sj,mkj->mks", radial_table, axial_coefficient, precision=forward_precision)
    scaled = spectrum / denominator_of(mode_ids, jnp.arange(NR, dtype=jnp.int32))
    radial_returned = jnp.einsum("sj,mks->mkj", radial_table, scaled, precision=maximal_precision)
    radial_returned = radial_returned.reshape(modes_each, NX, row_count, radial_block)
    physical_space = jnp.einsum(
        "kgx,mkrj->grmxj",
        jnp.asarray(AXIAL_TABLE).reshape(NX, gz_count, axial_block),
        radial_returned,
        precision=maximal_precision,
    )
    first_p = physical_space[:, :, :, :1]
    last_p = physical_space[:, :, :, -1:]
    ghost_low = jnp.concatenate([jnp.zeros_like(last_p[:1]), last_p[:-1]], axis=0)
    ghost_high = jnp.concatenate([first_p[1:], jnp.zeros_like(first_p[:1])], axis=0)
    windows = jnp.concatenate([physical_space, ghost_low, ghost_high], axis=3)
    windows = windows.reshape(device_count, modes_each, axial_block + 2, radial_block)
    returned = lax.all_to_all(windows, both, split_axis=0, concat_axis=0, tiled=True)
    extended_p = -jnp.einsum(
        "smxr,tsm->xrt",
        returned,
        fourier.reshape(NT, device_count, modes_each),
        precision=maximal_precision,
    )
    pressure = extended_p[:axial_block]
    padded = jnp.concatenate(
        [extended_p[axial_block : axial_block + 1], pressure, extended_p[axial_block + 1 :]], axis=0
    )
    if row_count == 2:
        sideways = radial_neighbour(pressure, pressure[:, :1], pressure[:, -1:])
        above = sideways[:, 2:]
        below = sideways[:, :-2]
    else:
        wide = extended(pressure, (("row", 1),), 1)
        lower_ghost = jnp.where(row_index == 0, pressure[:, :1], wide[:, :1])
        upper_ghost = jnp.where(row_index == row_count - 1, pressure[:, -1:], wide[:, -1:])
        above = jnp.concatenate([pressure[:, 1:], upper_ghost], axis=1)
        below = jnp.concatenate([lower_ghost, pressure[:, :-1]], axis=1)
    axial_out = axial_vel - 0.5 * (padded[2:] - padded[:-2])
    radial_projected_velocity = radial_vel - 0.5 * (above - below)
    swirl_out = swirl_vel - (jnp.roll(pressure, -1, 2) - jnp.roll(pressure, 1, 2)) / (
        2.0 * radius * spacing
    )
    return (axial_out, radial_projected_velocity, swirl_out)


def solution(mesh):
    placed = (
        P("gz", "row", None),
        P("gz", "row", None),
        P("gz", "row", None),
        P(),
        P("gz", "row", None),
    )
    return jax.shard_map(
        body,
        mesh=mesh,
        in_specs=placed,
        out_specs=(P("gz", "row", None), P("gz", "row", None), P("gz", "row", None)),
        check_vma=False,
    )
```

```python
import math

import numpy as np

import jax
import jax.numpy as jnp
from jax import lax
from jax.sharding import PartitionSpec as P

NX = 1024
NR = 256
NT = 256
GORES = 48


helmholtz_shift = 0.001
maximal_precision = lax.Precision.HIGHEST
forward_precision = lax.Precision.HIGH


def extended(block, sides, width):
    for axis, dim in sides:
        count = lax.axis_size(axis)
        forward = [(i, i + 1) for i in range(count - 1)]
        backward = [(target, source) for source, target in forward]
        low = lax.ppermute(
            lax.slice_in_dim(block, block.shape[dim] - width, None, axis=dim), axis, forward
        )
        high = lax.ppermute(lax.slice_in_dim(block, 0, width, axis=dim), axis, backward)
        block = jnp.concatenate([low, block, high], axis=dim)
    return block


def radial_neighbour(block, ghost_low, ghost_high):
    row_index = lax.axis_index("row")
    send = jnp.where(row_index == 0, block[:, -1:], block[:, :1])
    received = lax.ppermute(send, "row", [(0, 1), (1, 0)])
    low = jnp.where(row_index == 0, ghost_low, received)
    high = jnp.where(row_index == 0, received, ghost_high)
    return jnp.concatenate([low, block, high], axis=1)


def azimuth_basis(extent, mode_ids):
    positions = jnp.arange(extent, dtype=jnp.int32)
    half_way = extent // 2
    frequency = jnp.where(mode_ids <= half_way, mode_ids, mode_ids - half_way)
    phases = positions[:, None] * frequency[None, :] % extent
    angles = phases.astype(jnp.float32) * (2.0 * math.pi / extent)
    weights = jnp.where(
        (mode_ids == 0) | (mode_ids == half_way), math.sqrt(1.0 / extent), math.sqrt(2.0 / extent)
    ).astype(jnp.float32)
    return (
        jnp.where((mode_ids > half_way)[None, :], jnp.sin(angles), jnp.cos(angles))
        * weights[None, :]
    )


def azimuth_eigen(mode_ids):
    half_way = NT // 2
    frequency = jnp.where(mode_ids <= half_way, mode_ids, mode_ids - half_way)
    angles = frequency.astype(jnp.float32) * (2.0 * math.pi / NT)
    arc_step = 0.75 * NR * 2.0 * math.pi / NT
    return (2.0 - 2.0 * jnp.cos(angles)) / (arc_step * arc_step)


def axial_basis(extent):
    indices = jnp.arange(extent, dtype=jnp.int32) + 1
    phases = indices[:, None] * indices[None, :] % (2 * (extent + 1))
    angles = phases.astype(jnp.float32) * (math.pi / (extent + 1))
    return jnp.sin(angles) * math.sqrt(2.0 / (extent + 1))


def axial_eigen(extent):
    indices = jnp.arange(extent, dtype=jnp.int32) + 1
    return 2.0 - 2.0 * jnp.cos(indices.astype(jnp.float32) * (math.pi / (extent + 1)))


def radial_basis(extent):
    mode_ids = jnp.arange(extent, dtype=jnp.int32)[:, None]
    cell_ids = jnp.arange(extent, dtype=jnp.int32)[None, :]
    phases = mode_ids * (2 * cell_ids + 1) % (4 * extent)
    angles = phases.astype(jnp.float32) * (math.pi / (2 * extent))
    weights = jnp.where(mode_ids == 0, math.sqrt(1.0 / extent), math.sqrt(2.0 / extent)).astype(
        jnp.float32
    )
    return jnp.cos(angles) * weights


def radial_eigen(mode_ids):
    return 2.0 - 2.0 * jnp.cos(mode_ids.astype(jnp.float32) * (math.pi / NR))


def cell_radius(cell_ids):
    return cell_ids.astype(jnp.float32) + (0.25 * NR + 0.5)


def fixed_azimuth_basis():
    positions = np.arange(NT)[:, None]
    modes = np.arange(NT)[None, :]
    frequency = np.where(modes <= NT // 2, modes, modes - NT // 2)
    angles = (positions * frequency % NT) * (2.0 * math.pi / NT)
    weights = np.where((modes == 0) | (modes == NT // 2), math.sqrt(1.0 / NT), math.sqrt(2.0 / NT))
    return (np.where(modes > NT // 2, np.sin(angles), np.cos(angles)) * weights).astype(np.float32)


def fixed_axial_basis():
    indices = np.arange(1, NX + 1)
    phases = indices[:, None] * indices[None, :] % (2 * (NX + 1))
    return (np.sin(phases * (math.pi / (NX + 1))) * math.sqrt(2.0 / (NX + 1))).astype(np.float32)


def fixed_radial_basis():
    modes = np.arange(NR)[:, None]
    cells = np.arange(NR)[None, :]
    angles = (modes * (2 * cells + 1) % (4 * NR)) * (math.pi / (2 * NR))
    weights = np.where(modes == 0, math.sqrt(1.0 / NR), math.sqrt(2.0 / NR))
    return (np.cos(angles) * weights).astype(np.float32)


AZIMUTH_TABLE = fixed_azimuth_basis()
SHIFTED_TABLE = (np.roll(AZIMUTH_TABLE.astype(np.float64), 1, axis=0)
                 - np.roll(AZIMUTH_TABLE.astype(np.float64), -1, axis=0)).astype(np.float32)
AXIAL_TABLE = fixed_axial_basis()


def halo_axial_tables(blocks):
    width = NX // blocks
    table = AXIAL_TABLE.reshape(NX, blocks, width)
    zero = np.zeros((NX, 1), np.float32)
    below = np.concatenate([zero, AXIAL_TABLE[:, width - 1 : NX - 1 : width]], axis=1)
    above = np.concatenate([AXIAL_TABLE[:, width::width], zero], axis=1)
    forward = np.concatenate([table, 0.5 * below[:, :, None], -0.5 * above[:, :, None]], axis=2)
    inverse = np.concatenate([table, below[:, :, None], above[:, :, None]], axis=2)
    return forward.astype(np.float32), inverse.astype(np.float32)
RADIAL_TABLE = fixed_radial_basis()


def denominator_of(mode_ids, radial_ids):
    total = azimuth_eigen(mode_ids)[:, None, None] + axial_eigen(NX)[None, :, None]
    return total + radial_eigen(radial_ids)[None, None, :] + helmholtz_shift


def canopy_source(gore_map, rate_table):
    gore_ids = jnp.arange(rate_table.shape[0], dtype=jnp.int32)
    column_gore = jnp.arange(NT, dtype=jnp.int32) * GORES // NT
    matches = column_gore[:, None] == gore_ids[None, :]
    column_rate = jnp.sum(jnp.where(matches, rate_table[None, :], 0.0), axis=1)
    return jnp.where(gore_map < GORES, column_rate[None, None, :], 0.0)


def body(axial_vel, radial_vel, swirl_vel, inflow_rate, canopy_gore):
    radial_block = axial_vel.shape[1]
    axial_block = axial_vel.shape[0]
    row_index = lax.axis_index("row")
    row_count = lax.axis_size("row")
    gz_count = lax.axis_size("gz")
    both = ("gz", "row")
    device_count = gz_count * row_count
    spacing = 2.0 * math.pi / NT
    own_first = row_index * radial_block
    own_cells = own_first + jnp.arange(radial_block, dtype=jnp.int32)
    radius = cell_radius(own_cells)[None, :, None]
    axial_pad = jnp.pad(axial_vel, ((1, 1), (0, 0), (0, 0)))
    flux = radial_vel * radius
    if row_count == 2:
        no_flux = jnp.zeros_like(flux[:, :1])
        radial_flux = radial_neighbour(flux, no_flux, no_flux)
    else:
        radial_flux = extended(flux, (("row", 1),), 1)
    divergence = 0.5 * (axial_pad[2:] - axial_pad[:-2])
    divergence = divergence + (radial_flux[:, 2:] - radial_flux[:, :-2]) / (2.0 * radius)
    right_side = divergence - canopy_source(canopy_gore, inflow_rate)
    all_modes = jnp.arange(NT, dtype=jnp.int32)
    fourier = jnp.asarray(AZIMUTH_TABLE)
    planes = jnp.concatenate([right_side, axial_vel[:1], axial_vel[-1:]], axis=0)
    spectrum_in = jnp.einsum("xrt,tm->mxr", planes, fourier, precision=forward_precision)
    swirl_modes = jnp.einsum(
        "xrt,tm->mxr", swirl_vel, jnp.asarray(SHIFTED_TABLE), precision=forward_precision
    ) / (2.0 * radius[:, :, 0] * spacing)
    swirl_modes = jnp.concatenate([swirl_modes, jnp.zeros_like(swirl_modes[:, :2])], axis=1)
    spectrum_in = spectrum_in + swirl_modes
    modes_each = NT // device_count
    spectrum_in = spectrum_in.reshape(device_count, modes_each, axial_block + 2, radial_block)
    resident = lax.all_to_all(spectrum_in, both, split_axis=0, concat_axis=0, tiled=True)
    resident = resident.reshape(gz_count, row_count, modes_each, axial_block + 2, radial_block)
    mode_ids = lax.axis_index(both) * modes_each + jnp.arange(modes_each, dtype=jnp.int32)
    forward_table = halo_axial_tables(gz_count)[0]
    radial_table = jnp.asarray(RADIAL_TABLE)
    axial_coefficient = jnp.einsum(
        "kgx,grmxj->mkrj", jnp.asarray(forward_table), resident, precision=forward_precision
    ).reshape(modes_each, NX, NR)
    spectrum = jnp.einsum("sj,mkj->mks", radial_table, axial_coefficient, precision=forward_precision)
    scaled = spectrum / denominator_of(mode_ids, jnp.arange(NR, dtype=jnp.int32))
    radial_returned = jnp.einsum("sj,mks->mkj", radial_table, scaled, precision=maximal_precision)
    radial_returned = radial_returned.reshape(modes_each, NX, row_count, radial_block)
    physical_space = jnp.einsum(
        "kgx,mkrj->grmxj",
        jnp.asarray(AXIAL_TABLE).reshape(NX, gz_count, axial_block),
        radial_returned,
        precision=maximal_precision,
    )
    first_p = physical_space[:, :, :, :1]
    last_p = physical_space[:, :, :, -1:]
    ghost_low = jnp.concatenate([jnp.zeros_like(last_p[:1]), last_p[:-1]], axis=0)
    ghost_high = jnp.concatenate([first_p[1:], jnp.zeros_like(first_p[:1])], axis=0)
    windows = jnp.concatenate([physical_space, ghost_low, ghost_high], axis=3)
    windows = windows.reshape(device_count, modes_each, axial_block + 2, radial_block)
    returned = lax.all_to_all(windows, both, split_axis=0, concat_axis=0, tiled=True)
    extended_p = -jnp.einsum(
        "smxr,tsm->xrt",
        returned,
        fourier.reshape(NT, device_count, modes_each),
        precision=maximal_precision,
    )
    pressure = extended_p[:axial_block]
    padded = jnp.concatenate(
        [extended_p[axial_block : axial_block + 1], pressure, extended_p[axial_block + 1 :]], axis=0
    )
    if row_count == 2:
        sideways = radial_neighbour(pressure, pressure[:, :1], pressure[:, -1:])
        above = sideways[:, 2:]
        below = sideways[:, :-2]
    else:
        wide = extended(pressure, (("row", 1),), 1)
        lower_ghost = jnp.where(row_index == 0, pressure[:, :1], wide[:, :1])
        upper_ghost = jnp.where(row_index == row_count - 1, pressure[:, -1:], wide[:, -1:])
        above = jnp.concatenate([pressure[:, 1:], upper_ghost], axis=1)
        below = jnp.concatenate([lower_ghost, pressure[:, :-1]], axis=1)
    axial_out = axial_vel - 0.5 * (padded[2:] - padded[:-2])
    radial_projected_velocity = radial_vel - 0.5 * (above - below)
    swirl_out = swirl_vel - (jnp.roll(pressure, -1, 2) - jnp.roll(pressure, 1, 2)) / (
        2.0 * radius * spacing
    )
    return (axial_out, radial_projected_velocity, swirl_out)


def solution(mesh):
    placed = (
        P("gz", "row", None),
        P("gz", "row", None),
        P("gz", "row", None),
        P(),
        P("gz", "row", None),
    )
    return jax.shard_map(
        body,
        mesh=mesh,
        in_specs=placed,
        out_specs=(P("gz", "row", None), P("gz", "row", None), P("gz", "row", None)),
        check_vma=False,
    )
```
